128 devices in a mesh: slab: 32 (over z, y, core), cross: 4 (over x).
Axes of the slice: x: 4, y: 4, z: 4, core: 2. Of those that a mesh axis runs over, the one named last changes fastest.
Arguments:
- state: float32 [5, 64, 4096], P(None, 'slab', 'cross'), may hold values from -1.2 to 1.2
- rhs: float32 [5, 64, 4096], P(None, 'slab', 'cross'), may hold values from -1.2 to 1.2
- dinv: float32 [5, 5, 64, 4096], P(None, None, 'slab', 'cross'), may hold values from -0.3 to 2.3, as said below
- lower_jac: float32 [5, 5, 64, 4096], P(None, None, 'slab', 'cross'), may hold values from -0.3 to 2.3
- upper_jac: float32 [5, 5, 64, 4096], P(None, None, 'slab', 'cross'), may hold values from -0.3 to 2.3
- owner: int32 [131072, 1], P(('slab', 'cross')), may hold values from 0 to 127; in each aligned block of 1024 rows (0 to 1023, 1024 to 2047, ...) at most 32 rows name the same one
- donor_block: int32 [131072], P(('slab', 'cross')), may hold values from 0 to 15
- offsets: int32 [8, 131072], P(None, ('slab', 'cross')), may hold values from 0 to 127
- weights: float32 [8, 131072], P(None, ('slab', 'cross')), may hold values from 0 to 1, as said below
- receptor_perm: int32 [128, 16], P(('slab', 'cross')), may hold values from 0 to 15, each once within a row
Outputs:
- update: float32 [5, 64, 4096], P(None, 'slab', 'cross')
The draws below stay inside these ranges and needn't reach their ends.
Inputs may be any that keep to these rules, and one draw needn't show every extreme that they name: `dinv`: each is s (I + E) with s between 0.5 and 2 a cell and small E. `weights`: positive; the 8 weights of one fringe point sum to one. Among the 1024 fringe points of one device no owner is named more than 32 times.
All inputs are finite; a program needn't handle non-finite values.
Results may differ from the reference program's by a relative error of at most 0.00021.
Values sent between devices are 32-bit elements; how exact they have to be, the bound alone decides.
No kernel may reach another device: no remote copies, remote signals or barrier semaphores. Data moves between devices by JAX's collectives and lax.ppermute only.
A program may use at most 64 MiB of HBM per device.

```python
import math
import jax
import jax.numpy as jnp
import numpy as np
from jax import lax

VARIABLES = 5
CORNERS = 8
BLOCK_CELLS = 128
PLANES_DEV = 2
CELLS_DEV = 1024
BLOCKS_DEV = 16
FRINGE_BLOCKS = 8
FRINGE_DEV = 1024
CAPACITY = 32
LAYER_COUNT = 64
COLUMNS = 4096
FRINGE = 131072
N_SLAB = 32
N_CROSS = 4
DEVICES = 128


def cell_scale(key):
    draw = jax.random.uniform(jax.random.fold_in(key, 501), (LAYER_COUNT, COLUMNS), jnp.float32)
    return jnp.exp(jnp.log(0.5) + draw * jnp.log(4.0))


def channel_rates(key, salt):
    first, second, third, fourth = jax.random.split(jax.random.fold_in(key, salt), 4)
    lowest = jnp.log(20.0)
    highest = jnp.log(3.0 * LAYER_COUNT)
    life = jnp.exp(lowest + jax.random.uniform(first, (VARIABLES, 1, 1), jnp.float32) * (highest - lowest))
    life = life * jnp.exp(jax.random.uniform(second, (VARIABLES, LAYER_COUNT, COLUMNS), jnp.float32, -0.35, 0.35))
    damping_factor = jnp.exp(-1.0 / life)
    picked_elements = jax.random.randint(third, (3,), 0, LAYER_COUNT)
    traversal_batch_team = jnp.any(jnp.arange(LAYER_COUNT)[:, None] == picked_elements[None, :], axis=1)
    goal_measure = jax.random.uniform(fourth, (VARIABLES, 1, 1), jnp.float32, 0.5, 0.8)
    return jnp.where(traversal_batch_team[None, :, None], damping_factor * goal_measure, damping_factor)


def small_noise(key, salt):
    return 0.04 * jax.random.truncated_normal(jax.random.fold_in(key, salt), -3.0, 3.0, (VARIABLES, VARIABLES, LAYER_COUNT, COLUMNS), jnp.float32)


def identity_block():
    return jnp.eye(VARIABLES, dtype=jnp.float32)[:, :, None, None]


def draw_dinv(key, part):
    scale = cell_scale(key)
    return scale[None, None] * (identity_block() + small_noise(key, 601))


def draw_lower_jac(key, part):
    scale = cell_scale(key)
    damping_factor = channel_rates(key, 701)
    return (identity_block() * damping_factor[:, None] + small_noise(key, 702)) / scale[None, None]


def draw_upper_jac(key, part):
    scale = cell_scale(key)
    damping_factor = channel_rates(key, 801)
    return (identity_block() * damping_factor[:, None] + small_noise(key, 802)) / scale[None, None]


def draw_weights(key, part):
    raw = jax.random.uniform(jax.random.fold_in(key, 901), (CORNERS, FRINGE), jnp.float32, 0.05, 1.0)
    return raw / jnp.sum(raw, axis=0, keepdims=True)


def with_ends(values, stream_key, least, largest):
    place = [jax.random.randint(jax.random.fold_in(stream_key, axis), (), 0, length) for axis, length in enumerate(values.shape)]
    longest = values.shape.index(max(values.shape))
    beside = place[:longest] + [(place[longest] + 1) % values.shape[longest]] + place[longest + 1:]
    return values.at[tuple(place)].set(least).at[tuple(beside)].set(largest)


def block_scale(rng, dims, pieces, least, high):
    loudness = 1.0
    for axis_at, blocks in pieces:
        heights = jax.random.uniform(jax.random.fold_in(jax.random.fold_in(rng, 6), axis_at), (blocks,), jnp.float32, least / len(pieces), high / len(pieces))
        loudness = loudness * jnp.repeat(jnp.exp(heights), dims[axis_at] // blocks).reshape((-1,) + (1,) * (len(dims) - 1 - axis_at))
    return loudness


def shared_out(key, own, number, rows, count, top, bound, skew):
    sequence = jax.random.permutation(key, count)
    heavy_load, ordinary = shares(count, rows * top, bound, skew, True), shares(count, rows * top, bound, skew, False)
    places = jnp.arange(count)

    def named(tallies, offset_by):
        used = int((tallies > 0).sum())
        fixed = max(1, used // 4)
        passed = fixed + (places - fixed + offset_by * (used - fixed)) % max(1, count - fixed)
        return jnp.zeros((count,), jnp.int32).at[sequence[jnp.where(places < fixed, places, passed)]].set(jnp.asarray(tallies, jnp.int32))

    tallies = jnp.where(number % 4 == 0, named(heavy_load, number // 4), named(ordinary, number - number // 4 - 1))
    mixed = jax.random.permutation(jax.random.fold_in(own, 3), count)
    giver, taker = mixed[0:count // 2 * 2:2], mixed[1:count // 2 * 2:2]
    slack = jnp.minimum(tallies[giver] - 1, bound - tallies[taker]) // 2
    slack = jnp.where((giver == sequence[0]) | (taker == sequence[0]) | (tallies[taker] == 0), 0, jnp.maximum(slack, 0))
    passed = jax.random.randint(jax.random.fold_in(own, 4), (count // 2,), 0, 1 << 20) % (slack + 1)
    tallies = tallies.at[giver].add(-passed).at[taker].add(passed)
    labels = jnp.searchsorted(jnp.cumsum(tallies), jnp.arange(rows * top), side="right").astype(jnp.int32)
    table = labels.reshape(top, rows).T
    table = table[jax.random.permutation(jax.random.fold_in(own, 1), rows)]
    offset_by = jax.random.randint(jax.random.fold_in(own, 2), (rows, 1), 0, top)
    return jnp.take_along_axis(table, (jnp.arange(top)[None, :] + offset_by) % top, axis=1)


def shares(count, total, reach, lean, full):
    loads = [(1 << 20) // math.isqrt(grade ** lean) + 1 for grade in range(1, count + 1)]
    largest = reach if full else min(reach, max(-(-total // count), total * loads[0] // sum(loads)))
    least = 1 if total - largest >= count - 1 else 0
    given, spare = [largest] + [least] * (count - 1), total - largest - least * (count - 1)
    while spare > 0:
        free = [i for i in range(1, count) if given[i] < largest] or [i for i in range(1, count) if given[i] < reach]
        pool, left = sum([loads[i] for i in free]), spare
        for i in free:
            addition = min(reach - given[i], max(1, left * loads[i] // pool), spare)
            given[i] = given[i] + addition
            spare = spare - addition
    return np.array(given)


def scatter_about(key, dims, spread, most, pieces=(), kind=jnp.bfloat16):
    level = block_scale(key, dims, pieces, -0.22, 0.18) if pieces else 1.0
    values = jax.random.normal(key, dims, jnp.float32) * spread * level
    return jnp.minimum(jnp.maximum(values, -most), most).astype(kind)


def setup_inputs(seed: int = 0) -> dict:
    splits = jax.random.split(jax.random.key(seed), 11)
    state = scatter_about(splits[0], (VARIABLES, LAYER_COUNT, COLUMNS), 0.2, 1.2, ((1, 32), (2, 4)), jnp.float32)
    rhs = scatter_about(splits[1], (VARIABLES, LAYER_COUNT, COLUMNS), 0.2, 1.2, ((1, 32), (2, 4)), jnp.float32)
    dinv = draw_dinv(jax.random.fold_in(splits[10], 71), 0)
    lower_jac = draw_lower_jac(jax.random.fold_in(splits[10], 71), 0)
    upper_jac = draw_upper_jac(jax.random.fold_in(splits[10], 71), 0)
    owner_keys = jax.random.split(jax.random.fold_in(splits[5], 1), FRINGE // FRINGE_DEV)
    owner_turns = jax.random.permutation(jax.random.fold_in(splits[5], 3), FRINGE // FRINGE_DEV)
    owner = jax.vmap(lambda own, number: shared_out(jax.random.fold_in(splits[5], 2), own, number, FRINGE_DEV, DEVICES, 1, CAPACITY, 2))(owner_keys, owner_turns).reshape((FRINGE, 1))
    donor_block = with_ends(jax.random.randint(splits[6], (FRINGE,), 0, BLOCKS_DEV), jax.random.fold_in(splits[6], 1), 0, BLOCKS_DEV - 1).astype(jnp.int32)
    offsets = with_ends(jax.random.randint(splits[7], (CORNERS, FRINGE), 0, BLOCK_CELLS), jax.random.fold_in(splits[7], 1), 0, BLOCK_CELLS - 1).astype(jnp.int32)
    weights = draw_weights(jax.random.fold_in(splits[10], 71), 0)
    receptor_perm = jax.vmap(lambda own: jax.random.permutation(own, BLOCKS_DEV))(jax.random.split(splits[9], DEVICES)).reshape((DEVICES, BLOCKS_DEV)).astype(jnp.int32)
    return dict(state=state, rhs=rhs, dinv=dinv, lower_jac=lower_jac, upper_jac=upper_jac, owner=owner, donor_block=donor_block, offsets=offsets, weights=weights, receptor_perm=receptor_perm)


def onto_processors(field):
    width = field.shape[0]
    split = field.reshape(width, N_SLAB, PLANES_DEV, N_CROSS, CELLS_DEV)
    split = split.transpose(0, 1, 3, 2, 4)
    return split.reshape(width, N_SLAB * N_CROSS, PLANES_DEV * CELLS_DEV)


def from_devices(flat):
    width = flat.shape[0]
    split = flat.reshape(width, N_SLAB, N_CROSS, PLANES_DEV, CELLS_DEV)
    split = split.transpose(0, 1, 3, 2, 4)
    return split.reshape(width, LAYER_COUNT, COLUMNS)


def reference(state, rhs, dinv, lower_jac, upper_jac, owner, donor_block, offsets, weights, receptor_perm):
    highest = lax.Precision.HIGHEST
    state_dev = onto_processors(state)
    rhs_dev = onto_processors(rhs)
    donor_owner = owner[:, 0]
    donor_cells = donor_block[None, :] * BLOCK_CELLS + offsets
    values = state_dev[:, donor_owner[None, :], donor_cells]
    interp = jnp.sum(weights[None] * values, axis=1)
    interp = interp.reshape(VARIABLES, DEVICES, FRINGE_DEV)
    starts = receptor_perm[:, :FRINGE_BLOCKS] * BLOCK_CELLS
    targets = (starts[:, :, None] + jnp.arange(BLOCK_CELLS, dtype=jnp.int32)[None, None, :]).reshape(DEVICES, FRINGE_DEV)
    rows = jnp.arange(DEVICES, dtype=jnp.int32)[:, None]
    current = state_dev[:, rows, targets]
    forced = rhs_dev.at[:, rows, targets].set(interp - current)
    forcing = from_devices(forced)

    def planes_first(array):
        return jnp.moveaxis(array, -2, 0)

    def lower_step(prior_iterate, inputs):
        inverse, coupling, source = inputs
        inner = source + jnp.einsum('ijc,jc->ic', coupling, prior_iterate, precision=highest)
        now = jnp.einsum('ijc,jc->ic', inverse, inner, precision=highest)
        return now, now

    start = jnp.zeros((VARIABLES, COLUMNS), jnp.float32)
    _, lower = lax.scan(lower_step, start, (planes_first(dinv), planes_first(lower_jac), planes_first(forcing)))

    def upper_step(following, inputs):
        inverse, coupling, partial_value = inputs
        inner = jnp.einsum('ijc,jc->ic', coupling, following, precision=highest)
        now = partial_value + jnp.einsum('ijc,jc->ic', inverse, inner, precision=highest)
        return now, now

    _, result = lax.scan(upper_step, start, (planes_first(dinv), planes_first(upper_jac), lower), reverse=True)
    return jnp.moveaxis(result, 0, 1)
```

```python
import jax
import jax.numpy as jnp
from jax import lax
from jax.sharding import PartitionSpec as P

BLOCK_CELLS = 128
HIGHEST = lax.Precision.HIGHEST


def apply_block(matrix, vector):
    return jnp.sum(matrix * vector[None], axis=1)


def chain_blocks(later, earlier):
    return jnp.sum(later[:, :, None] * earlier[None], axis=1)


def slab_maps(dinv, coupling, order):
    transfer = None
    for index in order:
        step = chain_blocks(dinv[:, :, index], coupling[:, :, index])
        transfer = step if transfer is None else chain_blocks(step, transfer)
    return transfer


def fold_entry(maps, offsets, index, reverse):
    peers = maps.shape[0]
    value = jnp.zeros(offsets.shape[1:], offsets.dtype)
    order = range(peers - 1, -1, -1) if reverse else range(peers)
    for at in order:
        new = apply_block(maps[at], value) + offsets[at]
        reached = at > index if reverse else at < index
        value = jnp.where(reached, new, value)
    return value


def interpolate_at_owner(state_flat, request):
    width, resident = state_flat.shape
    blocks = resident // BLOCK_CELLS
    corners = (request.shape[0] - 1) // 2
    block = request[0]
    offs = request[1 : 1 + corners]
    wts = request[1 + corners :]
    lanes = lax.broadcasted_iota(jnp.float32, (BLOCK_CELLS, 1), 0)
    spread = jnp.zeros((BLOCK_CELLS, request.shape[1]), jnp.float32)
    for k in range(corners):
        spread = spread + jnp.where(offs[k][None, :] == lanes, wts[k][None, :], 0.0)
    table = state_flat.reshape(width, blocks, BLOCK_CELLS).transpose(1, 0, 2)
    table = table.reshape(blocks * width, BLOCK_CELLS)
    every = jnp.dot(table, spread, precision=HIGHEST).reshape(blocks, width, -1)
    ids = lax.broadcasted_iota(jnp.float32, (blocks, 1, 1), 0)
    return jnp.sum(jnp.where(block[None, None, :] == ids, every, 0.0), axis=0)


def body(
    state, rhs, dinv, lower_jac, upper_jac, owner, donor_block, offsets, weights, receptor_perm
):
    width, planes, cells = state.shape
    resident_cells = planes * cells
    state_flat = state.reshape(width, resident_cells)
    devices = lax.axis_size(("slab", "cross"))
    slab_index = lax.axis_index("slab")
    fringe_rows = owner.shape[0]
    capacity = 4 * fringe_rows // devices
    blocks = resident_cells // BLOCK_CELLS

    low_map = slab_maps(dinv, lower_jac, range(planes))
    up_map = slab_maps(dinv, upper_jac, range(planes - 1, -1, -1))
    maps = jnp.concatenate(
        [low_map.reshape(width * width, cells), up_map.reshape(width * width, cells)], axis=0
    )
    all_maps = lax.all_gather(maps, "slab")
    peers = all_maps.shape[0]
    all_maps = all_maps.reshape(peers, 2, width, width, cells)

    target = owner[:, 0]
    onehot = (target[:, None] == jnp.arange(devices, dtype=jnp.int32)[None, :]).astype(jnp.int32)
    slot = jnp.sum(jnp.cumsum(onehot, axis=0) * onehot, axis=1) - 1
    flat_slot = target * capacity + slot
    payload = jnp.concatenate(
        [donor_block[None, :].astype(jnp.float32), offsets.astype(jnp.float32), weights], axis=0
    )
    request = jnp.zeros((payload.shape[0], devices * capacity), jnp.float32)
    request = request.at[:, flat_slot].set(payload).reshape(-1, devices, capacity)
    received = lax.all_to_all(request, ("slab", "cross"), split_axis=1, concat_axis=1, tiled=True)
    answer = interpolate_at_owner(state_flat, received.reshape(received.shape[0], -1))
    answer = answer.reshape(width, devices, capacity)
    arrived = lax.all_to_all(answer, ("slab", "cross"), split_axis=1, concat_axis=1, tiled=True)
    interp = jnp.take(arrived.reshape(width, devices * capacity), flat_slot, axis=1)

    fringe_blocks = fringe_rows // BLOCK_CELLS
    chosen = receptor_perm[0, :fringe_blocks]
    hits = chosen[None, :] == jnp.arange(blocks, dtype=jnp.int32)[:, None]
    interp_blocks = interp.reshape(width, fringe_blocks, BLOCK_CELLS)
    placed = jnp.sum(
        jnp.where(hits[None, :, :, None], interp_blocks[:, None, :, :], 0.0), axis=2
    )
    state_blocks = state_flat.reshape(width, blocks, BLOCK_CELLS)
    rhs_blocks = rhs.reshape(width, blocks, BLOCK_CELLS)
    is_fringe = jnp.any(hits, axis=1)[None, :, None]
    forcing = jnp.where(is_fringe, placed - state_blocks, rhs_blocks)
    forcing = forcing.reshape(width, planes, cells)

    value = jnp.zeros((width, cells), jnp.float32)
    for index in range(planes):
        value = apply_block(
            dinv[:, :, index], forcing[:, index] + apply_block(lower_jac[:, :, index], value)
        )
    low_last = lax.all_gather(value, "slab")
    low_entry = fold_entry(all_maps[:, 0], low_last, slab_index, False)
    lower_planes = []
    value = low_entry
    for index in range(planes):
        value = apply_block(
            dinv[:, :, index], forcing[:, index] + apply_block(lower_jac[:, :, index], value)
        )
        lower_planes.append(value)

    value = jnp.zeros((width, cells), jnp.float32)
    for index in range(planes - 1, -1, -1):
        value = lower_planes[index] + apply_block(
            dinv[:, :, index], apply_block(upper_jac[:, :, index], value)
        )
    up_first = lax.all_gather(value, "slab")
    up_entry = fold_entry(all_maps[:, 1], up_first, slab_index, True)
    result = [None] * planes
    value = up_entry
    for index in range(planes - 1, -1, -1):
        value = lower_planes[index] + apply_block(
            dinv[:, :, index], apply_block(upper_jac[:, :, index], value)
        )
        result[index] = value
    return jnp.stack(result, axis=1)


def solution(mesh):
    return jax.shard_map(
        body,
        mesh=mesh,
        in_specs=(
            P(None, "slab", "cross"),
            P(None, "slab", "cross"),
            P(None, None, "slab", "cross"),
            P(None, None, "slab", "cross"),
            P(None, None, "slab", "cross"),
            P(("slab", "cross"), None),
            P(("slab", "cross")),
            P(None, ("slab", "cross")),
            P(None, ("slab", "cross")),
            P(("slab", "cross"), None),
        ),
        out_specs=P(None, "slab", "cross"),
        check_vma=False,
    )
```

```python
import jax
import jax.numpy as jnp
from jax import lax
from jax.sharding import PartitionSpec as P

BLOCK_CELLS = 128
HIGHEST = lax.Precision.HIGHEST


def apply_block(matrix, vector):
    return jnp.sum(matrix * vector[None], axis=1)


def chain_blocks(later, earlier):
    return jnp.sum(later[:, :, None] * earlier[None], axis=1)


def interpolate_at_owner(state_flat, request):
    width, resident = state_flat.shape
    blocks = resident // BLOCK_CELLS
    corners = (request.shape[0] - 1) // 2
    block = request[0]
    offs = request[1 : 1 + corners]
    wts = request[1 + corners :]
    lanes = lax.broadcasted_iota(jnp.float32, (BLOCK_CELLS, 1), 0)
    spread = jnp.zeros((BLOCK_CELLS, request.shape[1]), jnp.float32)
    for k in range(corners):
        spread = spread + jnp.where(offs[k][None, :] == lanes, wts[k][None, :], 0.0)
    table = state_flat.reshape(width, blocks, BLOCK_CELLS).transpose(1, 0, 2)
    table = table.reshape(blocks * width, BLOCK_CELLS)
    every = jnp.dot(table, spread, precision=HIGHEST).reshape(blocks, width, -1)
    ids = lax.broadcasted_iota(jnp.float32, (blocks, 1, 1), 0)
    return jnp.sum(jnp.where(block[None, None, :] == ids, every, 0.0), axis=0)


def row_apply(maps, at, base, vector):
    width = vector.shape[0]
    rows = []
    for i in range(width):
        total = maps[at, base + i * width] * vector[0]
        for j in range(1, width):
            total = total + maps[at, base + i * width + j] * vector[j]
        rows.append(total)
    return jnp.stack(rows)


def body(
    state, rhs, dinv, lower_jac, upper_jac, owner, donor_block, offsets, weights, receptor_perm
):
    width, planes, cells = state.shape
    resident_cells = planes * cells
    state_flat = state.reshape(width, resident_cells)
    devices = lax.axis_size(("slab", "cross"))
    slab_index = lax.axis_index("slab")
    fringe_rows = owner.shape[0]
    capacity = 4 * fringe_rows // devices
    blocks = resident_cells // BLOCK_CELLS
    square = width * width

    partial = []
    transfer = None
    for index in range(planes):
        step = chain_blocks(dinv[:, :, index], lower_jac[:, :, index])
        transfer = step if transfer is None else chain_blocks(step, transfer)
        partial.append(transfer)
    low_map = transfer
    up_steps = [chain_blocks(dinv[:, :, index], upper_jac[:, :, index]) for index in range(planes)]
    up_map = None
    response = partial[planes - 1]
    for index in range(planes - 1, -1, -1):
        up_map = up_steps[index] if up_map is None else chain_blocks(up_steps[index], up_map)
        if index < planes - 1:
            response = partial[index] + chain_blocks(up_steps[index], response)
    maps = jnp.concatenate(
        [m.reshape(square, cells) for m in (low_map, up_map, response)], axis=0
    )
    all_maps = lax.all_gather(maps, "slab")
    peers = all_maps.shape[0]

    target = owner[:, 0]
    onehot = (target[:, None] == jnp.arange(devices, dtype=jnp.int32)[None, :]).astype(jnp.int32)
    slot = jnp.sum(jnp.cumsum(onehot, axis=0) * onehot, axis=1) - 1
    flat_slot = target * capacity + slot
    payload = jnp.concatenate(
        [donor_block[None, :].astype(jnp.float32), offsets.astype(jnp.float32), weights], axis=0
    )
    request = jnp.zeros((payload.shape[0], devices * capacity), jnp.float32)
    request = request.at[:, flat_slot].set(payload).reshape(-1, devices, capacity)
    received = lax.all_to_all(request, ("slab", "cross"), split_axis=1, concat_axis=1, tiled=True)
    answer = interpolate_at_owner(state_flat, received.reshape(received.shape[0], -1))
    answer = answer.reshape(width, devices, capacity)
    arrived = lax.all_to_all(answer, ("slab", "cross"), split_axis=1, concat_axis=1, tiled=True)
    interp = jnp.take(arrived.reshape(width, devices * capacity), flat_slot, axis=1)

    fringe_blocks = fringe_rows // BLOCK_CELLS
    chosen = receptor_perm[0, :fringe_blocks]
    hits = chosen[None, :] == jnp.arange(blocks, dtype=jnp.int32)[:, None]
    interp_blocks = interp.reshape(width, fringe_blocks, BLOCK_CELLS)
    placed = jnp.sum(
        jnp.where(hits[None, :, :, None], interp_blocks[:, None, :, :], 0.0), axis=2
    )
    state_blocks = state_flat.reshape(width, blocks, BLOCK_CELLS)
    rhs_blocks = rhs.reshape(width, blocks, BLOCK_CELLS)
    is_fringe = jnp.any(hits, axis=1)[None, :, None]
    forcing = jnp.where(is_fringe, placed - state_blocks, rhs_blocks)
    forcing = forcing.reshape(width, planes, cells)

    zero_lower = []
    value = jnp.zeros((width, cells), jnp.float32)
    for index in range(planes):
        value = apply_block(
            dinv[:, :, index], forcing[:, index] + apply_block(lower_jac[:, :, index], value)
        )
        zero_lower.append(value)
    value = jnp.zeros((width, cells), jnp.float32)
    for index in range(planes - 1, -1, -1):
        value = zero_lower[index] + apply_block(
            dinv[:, :, index], apply_block(upper_jac[:, :, index], value)
        )
    offsets_here = jnp.concatenate([zero_lower[planes - 1], value], axis=0)
    spread = jnp.broadcast_to(offsets_here[None], (peers,) + offsets_here.shape)
    every = lax.all_to_all(spread, "slab", 0, 0, tiled=True)

    entry = jnp.zeros((width, cells), jnp.float32)
    low_entry = entry
    up_offsets = []
    for at in range(peers):
        low_entry = jnp.where(at == slab_index, entry, low_entry)
        up_offsets.append(every[at, width:] + row_apply(all_maps, at, 2 * square, entry))
        entry = row_apply(all_maps, at, 0, entry) + every[at, :width]
    entry = jnp.zeros((width, cells), jnp.float32)
    up_entry = entry
    for at in range(peers - 1, -1, -1):
        up_entry = jnp.where(at == slab_index, entry, up_entry)
        entry = row_apply(all_maps, at, square, entry) + up_offsets[at]

    lower_planes = []
    value = low_entry
    for index in range(planes):
        value = apply_block(
            dinv[:, :, index], forcing[:, index] + apply_block(lower_jac[:, :, index], value)
        )
        lower_planes.append(value)
    result = [None] * planes
    value = up_entry
    for index in range(planes - 1, -1, -1):
        value = lower_planes[index] + apply_block(
            dinv[:, :, index], apply_block(upper_jac[:, :, index], value)
        )
        result[index] = value
    return jnp.stack(result, axis=1)


def solution(mesh):
    return jax.shard_map(
        body,
        mesh=mesh,
        in_specs=(
            P(None, "slab", "cross"),
            P(None, "slab", "cross"),
            P(None, None, "slab", "cross"),
            P(None, None, "slab", "cross"),
            P(None, None, "slab", "cross"),
            P(("slab", "cross"), None),
            P(("slab", "cross")),
            P(None, ("slab", "cross")),
            P(None, ("slab", "cross")),
            P(("slab", "cross"), None),
        ),
        out_specs=P(None, "slab", "cross"),
        check_vma=False,
    )
```

```python
import jax
import jax.numpy as jnp
from jax import lax
from jax.sharding import PartitionSpec as P

BLOCK_CELLS = 128
HIGHEST = lax.Precision.HIGHEST


def apply_block(matrix, vector):
    return jnp.sum(matrix * vector[None], axis=1)


def chain_blocks(later, earlier):
    return jnp.sum(later[:, :, None] * earlier[None], axis=1)


def interpolate_at_owner(state_flat, request):
    width, resident = state_flat.shape
    blocks = resident // BLOCK_CELLS
    corners = (request.shape[0] - 1) // 2
    block = request[0]
    offs = request[1 : 1 + corners]
    wts = request[1 + corners :]
    lanes = lax.broadcasted_iota(jnp.float32, (BLOCK_CELLS, 1), 0)
    spread = jnp.zeros((BLOCK_CELLS, request.shape[1]), jnp.float32)
    for k in range(corners):
        spread = spread + jnp.where(offs[k][None, :] == lanes, wts[k][None, :], 0.0)
    table = state_flat.reshape(width, blocks, BLOCK_CELLS).transpose(1, 0, 2)
    table = table.reshape(blocks * width, BLOCK_CELLS)
    every = jnp.dot(table, spread, precision=HIGHEST).reshape(blocks, width, -1)
    ids = lax.broadcasted_iota(jnp.float32, (blocks, 1, 1), 0)
    return jnp.sum(jnp.where(block[None, None, :] == ids, every, 0.0), axis=0)


def body(
    state, rhs, dinv, lower_jac, upper_jac, owner, donor_block, offsets, weights, receptor_perm
):
    width, planes, cells = state.shape
    resident_cells = planes * cells
    state_flat = state.reshape(width, resident_cells)
    devices = lax.axis_size(("slab", "cross"))
    slab_index = lax.axis_index("slab")
    fringe_rows = owner.shape[0]
    capacity = 4 * fringe_rows // devices
    blocks = resident_cells // BLOCK_CELLS
    square = width * width

    partial = []
    transfer = None
    for index in range(planes):
        step = chain_blocks(dinv[:, :, index], lower_jac[:, :, index])
        transfer = step if transfer is None else chain_blocks(step, transfer)
        partial.append(transfer)
    low_map = transfer
    up_steps = [chain_blocks(dinv[:, :, index], upper_jac[:, :, index]) for index in range(planes)]
    up_map = None
    response = partial[planes - 1]
    for index in range(planes - 1, -1, -1):
        up_map = up_steps[index] if up_map is None else chain_blocks(up_steps[index], up_map)
        if index < planes - 1:
            response = partial[index] + chain_blocks(up_steps[index], response)
    tile = (cells // BLOCK_CELLS, BLOCK_CELLS)
    maps = jnp.concatenate(
        [m.reshape((square,) + tile) for m in (low_map, up_map, response)], axis=0
    )
    all_maps = lax.all_gather(maps, "slab")
    peers = all_maps.shape[0]
    all_maps = all_maps.reshape((peers, 3, width, width) + tile)

    target = owner[:, 0]
    onehot = (target[:, None] == jnp.arange(devices, dtype=jnp.int32)[None, :]).astype(jnp.int32)
    slot = jnp.sum(jnp.cumsum(onehot, axis=0) * onehot, axis=1) - 1
    flat_slot = target * capacity + slot
    payload = jnp.concatenate(
        [donor_block[None, :].astype(jnp.float32), offsets.astype(jnp.float32), weights], axis=0
    )
    request = jnp.zeros((payload.shape[0], devices * capacity), jnp.float32)
    request = request.at[:, flat_slot].set(payload).reshape(-1, devices, capacity)
    received = lax.all_to_all(request, ("slab", "cross"), split_axis=1, concat_axis=1, tiled=True)
    answer = interpolate_at_owner(state_flat, received.reshape(received.shape[0], -1))
    answer = answer.reshape(width, devices, capacity)
    arrived = lax.all_to_all(answer, ("slab", "cross"), split_axis=1, concat_axis=1, tiled=True)
    interp = jnp.take(arrived.reshape(width, devices * capacity), flat_slot, axis=1)

    fringe_blocks = fringe_rows // BLOCK_CELLS
    chosen = receptor_perm[0, :fringe_blocks]
    hits = chosen[None, :] == jnp.arange(blocks, dtype=jnp.int32)[:, None]
    interp_blocks = interp.reshape(width, fringe_blocks, BLOCK_CELLS)
    placed = jnp.sum(
        jnp.where(hits[None, :, :, None], interp_blocks[:, None, :, :], 0.0), axis=2
    )
    state_blocks = state_flat.reshape(width, blocks, BLOCK_CELLS)
    rhs_blocks = rhs.reshape(width, blocks, BLOCK_CELLS)
    is_fringe = jnp.any(hits, axis=1)[None, :, None]
    forcing = jnp.where(is_fringe, placed - state_blocks, rhs_blocks)
    forcing = forcing.reshape(width, planes, cells)

    zero_lower = []
    value = jnp.zeros((width, cells), jnp.float32)
    for index in range(planes):
        value = apply_block(
            dinv[:, :, index], forcing[:, index] + apply_block(lower_jac[:, :, index], value)
        )
        zero_lower.append(value)
    value = jnp.zeros((width, cells), jnp.float32)
    for index in range(planes - 1, -1, -1):
        value = zero_lower[index] + apply_block(
            dinv[:, :, index], apply_block(upper_jac[:, :, index], value)
        )
    offsets_here = jnp.stack([zero_lower[planes - 1], value]).reshape((2, width) + tile)
    spread = jnp.broadcast_to(offsets_here[None], (peers,) + offsets_here.shape)
    every = lax.all_to_all(spread, "slab", 0, 0, tiled=True)

    entry = jnp.zeros((width,) + tile, jnp.float32)
    low_entry = entry
    up_offsets = []
    for at in range(peers):
        low_entry = jnp.where(at == slab_index, entry, low_entry)
        up_offsets.append(every[at, 1] + apply_block(all_maps[at, 2], entry))
        entry = apply_block(all_maps[at, 0], entry) + every[at, 0]
    entry = jnp.zeros((width,) + tile, jnp.float32)
    up_entry = entry
    for at in range(peers - 1, -1, -1):
        up_entry = jnp.where(at == slab_index, entry, up_entry)
        entry = apply_block(all_maps[at, 1], entry) + up_offsets[at]
    low_entry = low_entry.reshape(width, cells)
    up_entry = up_entry.reshape(width, cells)

    lower_planes = []
    value = low_entry
    for index in range(planes):
        value = apply_block(
            dinv[:, :, index], forcing[:, index] + apply_block(lower_jac[:, :, index], value)
        )
        lower_planes.append(value)
    result = [None] * planes
    value = up_entry
    for index in range(planes - 1, -1, -1):
        value = lower_planes[index] + apply_block(
            dinv[:, :, index], apply_block(upper_jac[:, :, index], value)
        )
        result[index] = value
    return jnp.stack(result, axis=1)


def solution(mesh):
    return jax.shard_map(
        body,
        mesh=mesh,
        in_specs=(
            P(None, "slab", "cross"),
            P(None, "slab", "cross"),
            P(None, None, "slab", "cross"),
            P(None, None, "slab", "cross"),
            P(None, None, "slab", "cross"),
            P(("slab", "cross"), None),
            P(("slab", "cross")),
            P(None, ("slab", "cross")),
            P(None, ("slab", "cross")),
            P(("slab", "cross"), None),
        ),
        out_specs=P(None, "slab", "cross"),
        check_vma=False,
    )
```

```python
import jax
import jax.numpy as jnp
from jax import lax
from jax.experimental import pallas as pl
from jax.experimental.pallas import tpu as pltpu
from jax.sharding import PartitionSpec as P

BLOCK_CELLS = 128
HIGHEST = lax.Precision.HIGHEST


def apply_block(matrix, vector):
    return jnp.sum(matrix * vector[None], axis=1)


def chain_blocks(later, earlier):
    return jnp.sum(later[:, :, None] * earlier[None], axis=1)


def interpolate_at_owner(state_flat, request):
    width, resident = state_flat.shape
    blocks = resident // BLOCK_CELLS
    corners = (request.shape[0] - 1) // 2
    block = request[0]
    offs = request[1 : 1 + corners]
    wts = request[1 + corners :]
    lanes = lax.broadcasted_iota(jnp.float32, (BLOCK_CELLS, 1), 0)
    spread = jnp.zeros((BLOCK_CELLS, request.shape[1]), jnp.float32)
    for k in range(corners):
        spread = spread + jnp.where(offs[k][None, :] == lanes, wts[k][None, :], 0.0)
    table = state_flat.reshape(width, blocks, BLOCK_CELLS).transpose(1, 0, 2)
    table = table.reshape(blocks * width, BLOCK_CELLS)
    every = jnp.dot(table, spread, precision=HIGHEST).reshape(blocks, width, -1)
    ids = lax.broadcasted_iota(jnp.float32, (blocks, 1, 1), 0)
    return jnp.sum(jnp.where(block[None, None, :] == ids, every, 0.0), axis=0)


def fold_kernel(index_ref, maps_ref, offsets_ref, out_ref, up_ref):
    peers = maps_ref.shape[0]
    width = out_ref.shape[1]
    square = width * width
    here = index_ref[0]
    zero = offsets_ref[0, 0] * 0.0

    def matvec(at, base, vector):
        rows = []
        for i in range(width):
            total = maps_ref[at, base + i * width] * vector[0]
            for j in range(1, width):
                total = total + maps_ref[at, base + i * width + j] * vector[j]
            rows.append(total)
        return rows

    def lower_step(at, carry):
        entry, kept = carry
        hit = at == here
        kept = tuple(jnp.where(hit, e, k) for e, k in zip(entry, kept))
        response = matvec(at, 2 * square, entry)
        for i in range(width):
            up_ref[at, i] = offsets_ref[at, width + i] + response[i]
        moved = matvec(at, 0, entry)
        entry = tuple(moved[i] + offsets_ref[at, i] for i in range(width))
        return entry, kept

    start = (tuple([zero] * width), tuple([zero] * width))
    _, low = lax.fori_loop(0, peers, lower_step, start)

    def upper_step(step, carry):
        at = peers - 1 - step
        entry, kept = carry
        hit = at == here
        kept = tuple(jnp.where(hit, e, k) for e, k in zip(entry, kept))
        moved = matvec(at, square, entry)
        entry = tuple(moved[i] + up_ref[at, i] for i in range(width))
        return entry, kept

    _, up = lax.fori_loop(0, peers, upper_step, start)
    for i in range(width):
        out_ref[0, i] = low[i]
        out_ref[1, i] = up[i]


def fold_entries(index, all_maps, every):
    peers, _, sub, lanes = all_maps.shape
    width = every.shape[1] // 2
    vmem = pltpu.MemorySpace.VMEM
    return pl.pallas_call(
        fold_kernel,
        out_shape=jax.ShapeDtypeStruct((2, width, sub, lanes), jnp.float32),
        in_specs=[
            pl.BlockSpec(memory_space=pltpu.MemorySpace.SMEM),
            pl.BlockSpec(memory_space=vmem),
            pl.BlockSpec(memory_space=vmem),
        ],
        out_specs=pl.BlockSpec(memory_space=vmem),
        scratch_shapes=[pltpu.VMEM((peers, width, sub, lanes), jnp.float32)],
        compiler_params=pltpu.CompilerParams(vmem_limit_bytes=48 * 1024 * 1024),
    )(index, all_maps, every)


def body(
    state, rhs, dinv, lower_jac, upper_jac, owner, donor_block, offsets, weights, receptor_perm
):
    width, planes, cells = state.shape
    resident_cells = planes * cells
    state_flat = state.reshape(width, resident_cells)
    devices = lax.axis_size(("slab", "cross"))
    slab_index = lax.axis_index("slab")
    fringe_rows = owner.shape[0]
    capacity = 4 * fringe_rows // devices
    blocks = resident_cells // BLOCK_CELLS
    square = width * width

    partial = []
    transfer = None
    for index in range(planes):
        step = chain_blocks(dinv[:, :, index], lower_jac[:, :, index])
        transfer = step if transfer is None else chain_blocks(step, transfer)
        partial.append(transfer)
    low_map = transfer
    up_steps = [chain_blocks(dinv[:, :, index], upper_jac[:, :, index]) for index in range(planes)]
    up_map = None
    response = partial[planes - 1]
    for index in range(planes - 1, -1, -1):
        up_map = up_steps[index] if up_map is None else chain_blocks(up_steps[index], up_map)
        if index < planes - 1:
            response = partial[index] + chain_blocks(up_steps[index], response)
    tile = (cells // BLOCK_CELLS, BLOCK_CELLS)
    maps = jnp.concatenate(
        [m.reshape((square,) + tile) for m in (low_map, up_map, response)], axis=0
    )
    all_maps = lax.all_gather(maps, "slab")
    peers = all_maps.shape[0]

    target = owner[:, 0]
    onehot = (target[:, None] == jnp.arange(devices, dtype=jnp.int32)[None, :]).astype(jnp.int32)
    slot = jnp.sum(jnp.cumsum(onehot, axis=0) * onehot, axis=1) - 1
    flat_slot = target * capacity + slot
    payload = jnp.concatenate(
        [donor_block[None, :].astype(jnp.float32), offsets.astype(jnp.float32), weights], axis=0
    )
    request = jnp.zeros((payload.shape[0], devices * capacity), jnp.float32)
    request = request.at[:, flat_slot].set(payload).reshape(-1, devices, capacity)
    received = lax.all_to_all(request, ("slab", "cross"), split_axis=1, concat_axis=1, tiled=True)
    answer = interpolate_at_owner(state_flat, received.reshape(received.shape[0], -1))
    answer = answer.reshape(width, devices, capacity)
    arrived = lax.all_to_all(answer, ("slab", "cross"), split_axis=1, concat_axis=1, tiled=True)
    interp = jnp.take(arrived.reshape(width, devices * capacity), flat_slot, axis=1)

    fringe_blocks = fringe_rows // BLOCK_CELLS
    chosen = receptor_perm[0, :fringe_blocks]
    hits = chosen[None, :] == jnp.arange(blocks, dtype=jnp.int32)[:, None]
    interp_blocks = interp.reshape(width, fringe_blocks, BLOCK_CELLS)
    placed = jnp.sum(
        jnp.where(hits[None, :, :, None], interp_blocks[:, None, :, :], 0.0), axis=2
    )
    state_blocks = state_flat.reshape(width, blocks, BLOCK_CELLS)
    rhs_blocks = rhs.reshape(width, blocks, BLOCK_CELLS)
    is_fringe = jnp.any(hits, axis=1)[None, :, None]
    forcing = jnp.where(is_fringe, placed - state_blocks, rhs_blocks)
    forcing = forcing.reshape(width, planes, cells)

    zero_lower = []
    value = jnp.zeros((width, cells), jnp.float32)
    for index in range(planes):
        value = apply_block(
            dinv[:, :, index], forcing[:, index] + apply_block(lower_jac[:, :, index], value)
        )
        zero_lower.append(value)
    value = jnp.zeros((width, cells), jnp.float32)
    for index in range(planes - 1, -1, -1):
        value = zero_lower[index] + apply_block(
            dinv[:, :, index], apply_block(upper_jac[:, :, index], value)
        )
    offsets_here = jnp.stack([zero_lower[planes - 1], value]).reshape((2, width) + tile)
    spread = jnp.broadcast_to(offsets_here[None], (peers,) + offsets_here.shape)
    every = lax.all_to_all(spread, "slab", 0, 0, tiled=True)

    every = every.reshape((peers, 2 * width) + tile)
    index = jnp.reshape(slab_index, (1,)).astype(jnp.int32)
    entries = fold_entries(index, all_maps, every).reshape(2, width, cells)
    low_entry = entries[0]
    up_entry = entries[1]

    lower_planes = []
    value = low_entry
    for index in range(planes):
        value = apply_block(
            dinv[:, :, index], forcing[:, index] + apply_block(lower_jac[:, :, index], value)
        )
        lower_planes.append(value)
    result = [None] * planes
    value = up_entry
    for index in range(planes - 1, -1, -1):
        value = lower_planes[index] + apply_block(
            dinv[:, :, index], apply_block(upper_jac[:, :, index], value)
        )
        result[index] = value
    return jnp.stack(result, axis=1)


def solution(mesh):
    return jax.shard_map(
        body,
        mesh=mesh,
        in_specs=(
            P(None, "slab", "cross"),
            P(None, "slab", "cross"),
            P(None, None, "slab", "cross"),
            P(None, None, "slab", "cross"),
            P(None, None, "slab", "cross"),
            P(("slab", "cross"), None),
            P(("slab", "cross")),
            P(None, ("slab", "cross")),
            P(None, ("slab", "cross")),
            P(("slab", "cross"), None),
        ),
        out_specs=P(None, "slab", "cross"),
        check_vma=False,
    )
```

```python
import jax
import jax.numpy as jnp
from jax import lax
from jax.experimental import pallas as pl
from jax.experimental.pallas import tpu as pltpu
from jax.sharding import PartitionSpec as P

BLOCK_CELLS = 128
HIGHEST = lax.Precision.HIGHEST


def apply_block(matrix, vector):
    return jnp.sum(matrix * vector[None], axis=1)


def chain_blocks(later, earlier):
    return jnp.sum(later[:, :, None] * earlier[None], axis=1)


def interpolate_at_owner(state_flat, request):
    width, resident = state_flat.shape
    blocks = resident // BLOCK_CELLS
    corners = (request.shape[0] - 1) // 2
    block = request[0]
    offs = request[1 : 1 + corners]
    wts = request[1 + corners :]
    lanes = lax.broadcasted_iota(jnp.float32, (BLOCK_CELLS, 1), 0)
    spread = jnp.zeros((BLOCK_CELLS, request.shape[1]), jnp.float32)
    for k in range(corners):
        spread = spread + jnp.where(offs[k][None, :] == lanes, wts[k][None, :], 0.0)
    table = state_flat.reshape(width, blocks, BLOCK_CELLS).transpose(1, 0, 2)
    table = table.reshape(blocks * width, BLOCK_CELLS)
    every = jnp.dot(table, spread, precision=lax.Precision.HIGH).reshape(blocks, width, -1)
    ids = lax.broadcasted_iota(jnp.float32, (blocks, 1, 1), 0)
    return jnp.sum(jnp.where(block[None, None, :] == ids, every, 0.0), axis=0)


def fold_kernel(index_ref, maps_ref, offsets_ref, out_ref, up_ref):
    peers = maps_ref.shape[0]
    width = out_ref.shape[1]
    square = width * width
    here = index_ref[0]
    zero = offsets_ref[0, 0] * 0.0

    def matvec(at, base, vector):
        rows = []
        for i in range(width):
            total = maps_ref[at, base + i * width] * vector[0]
            for j in range(1, width):
                total = total + maps_ref[at, base + i * width + j] * vector[j]
            rows.append(total)
        return rows

    def lower_step(at, carry):
        entry, kept = carry
        hit = at == here
        kept = tuple(jnp.where(hit, e, k) for e, k in zip(entry, kept))
        response = matvec(at, 2 * square, entry)
        for i in range(width):
            up_ref[at, i] = offsets_ref[at, width + i] + response[i]
        moved = matvec(at, 0, entry)
        entry = tuple(moved[i] + offsets_ref[at, i] for i in range(width))
        return entry, kept

    start = (tuple([zero] * width), tuple([zero] * width))
    _, low = lax.fori_loop(0, peers, lower_step, start)

    def upper_step(step, carry):
        at = peers - 1 - step
        entry, kept = carry
        hit = at == here
        kept = tuple(jnp.where(hit, e, k) for e, k in zip(entry, kept))
        moved = matvec(at, square, entry)
        entry = tuple(moved[i] + up_ref[at, i] for i in range(width))
        return entry, kept

    _, up = lax.fori_loop(0, peers, upper_step, start)
    for i in range(width):
        out_ref[0, i] = low[i]
        out_ref[1, i] = up[i]


def fold_entries(index, all_maps, every):
    peers, _, sub, lanes = all_maps.shape
    width = every.shape[1] // 2
    vmem = pltpu.MemorySpace.VMEM
    return pl.pallas_call(
        fold_kernel,
        out_shape=jax.ShapeDtypeStruct((2, width, sub, lanes), jnp.float32),
        in_specs=[
            pl.BlockSpec(memory_space=pltpu.MemorySpace.SMEM),
            pl.BlockSpec(memory_space=vmem),
            pl.BlockSpec(memory_space=vmem),
        ],
        out_specs=pl.BlockSpec(memory_space=vmem),
        scratch_shapes=[pltpu.VMEM((peers, width, sub, lanes), jnp.float32)],
        compiler_params=pltpu.CompilerParams(vmem_limit_bytes=48 * 1024 * 1024),
    )(index, all_maps, every)


def body(
    state, rhs, dinv, lower_jac, upper_jac, owner, donor_block, offsets, weights, receptor_perm
):
    width, planes, cells = state.shape
    resident_cells = planes * cells
    state_flat = state.reshape(width, resident_cells)
    devices = lax.axis_size(("slab", "cross"))
    slab_index = lax.axis_index("slab")
    fringe_rows = owner.shape[0]
    capacity = 4 * fringe_rows // devices
    blocks = resident_cells // BLOCK_CELLS
    square = width * width

    partial = []
    transfer = None
    for index in range(planes):
        step = chain_blocks(dinv[:, :, index], lower_jac[:, :, index])
        transfer = step if transfer is None else chain_blocks(step, transfer)
        partial.append(transfer)
    low_map = transfer
    up_steps = [chain_blocks(dinv[:, :, index], upper_jac[:, :, index]) for index in range(planes)]
    up_map = None
    response = partial[planes - 1]
    for index in range(planes - 1, -1, -1):
        up_map = up_steps[index] if up_map is None else chain_blocks(up_steps[index], up_map)
        if index < planes - 1:
            response = partial[index] + chain_blocks(up_steps[index], response)
    tile = (cells // BLOCK_CELLS, BLOCK_CELLS)
    maps = jnp.concatenate(
        [m.reshape((square,) + tile) for m in (low_map, up_map, response)], axis=0
    )
    all_maps = lax.all_gather(maps, "slab")
    peers = all_maps.shape[0]

    target = owner[:, 0]
    onehot = (target[:, None] == jnp.arange(devices, dtype=jnp.int32)[None, :]).astype(jnp.int32)
    slot = jnp.sum(jnp.cumsum(onehot, axis=0) * onehot, axis=1) - 1
    flat_slot = target * capacity + slot
    payload = jnp.concatenate(
        [donor_block[None, :].astype(jnp.float32), offsets.astype(jnp.float32), weights], axis=0
    )
    rows = payload.shape[0]
    columns = jnp.arange(rows, dtype=jnp.int32)[None, :] * capacity + slot[:, None]
    request = jnp.zeros((devices, rows * capacity), jnp.float32)
    request = request.at[target[:, None], columns].set(payload.T)
    received = lax.all_to_all(request, ("slab", "cross"), split_axis=0, concat_axis=0, tiled=True)
    received = received.reshape(devices, rows, capacity).transpose(1, 0, 2)
    answer = interpolate_at_owner(state_flat, received.reshape(rows, devices * capacity))
    answer = answer.reshape(width, devices, capacity)
    arrived = lax.all_to_all(answer, ("slab", "cross"), split_axis=1, concat_axis=1, tiled=True)
    interp = jnp.take(arrived.reshape(width, devices * capacity), flat_slot, axis=1)

    fringe_blocks = fringe_rows // BLOCK_CELLS
    chosen = receptor_perm[0, :fringe_blocks]
    hits = chosen[None, :] == jnp.arange(blocks, dtype=jnp.int32)[:, None]
    interp_blocks = interp.reshape(width, fringe_blocks, BLOCK_CELLS)
    placed = jnp.sum(
        jnp.where(hits[None, :, :, None], interp_blocks[:, None, :, :], 0.0), axis=2
    )
    state_blocks = state_flat.reshape(width, blocks, BLOCK_CELLS)
    rhs_blocks = rhs.reshape(width, blocks, BLOCK_CELLS)
    is_fringe = jnp.any(hits, axis=1)[None, :, None]
    forcing = jnp.where(is_fringe, placed - state_blocks, rhs_blocks)
    forcing = forcing.reshape(width, planes, cells)

    zero_lower = []
    value = jnp.zeros((width, cells), jnp.float32)
    for index in range(planes):
        value = apply_block(
            dinv[:, :, index], forcing[:, index] + apply_block(lower_jac[:, :, index], value)
        )
        zero_lower.append(value)
    value = jnp.zeros((width, cells), jnp.float32)
    for index in range(planes - 1, -1, -1):
        value = zero_lower[index] + apply_block(
            dinv[:, :, index], apply_block(upper_jac[:, :, index], value)
        )
    offsets_here = jnp.stack([zero_lower[planes - 1], value]).reshape((2, width) + tile)
    spread = jnp.broadcast_to(offsets_here[None], (peers,) + offsets_here.shape)
    every = lax.all_to_all(spread, "slab", 0, 0, tiled=True)

    every = every.reshape((peers, 2 * width) + tile)
    index = jnp.reshape(slab_index, (1,)).astype(jnp.int32)
    entries = fold_entries(index, all_maps, every).reshape(2, width, cells)
    low_entry = entries[0]
    up_entry = entries[1]

    lower_planes = []
    value = low_entry
    for index in range(planes):
        value = apply_block(
            dinv[:, :, index], forcing[:, index] + apply_block(lower_jac[:, :, index], value)
        )
        lower_planes.append(value)
    result = [None] * planes
    value = up_entry
    for index in range(planes - 1, -1, -1):
        value = lower_planes[index] + apply_block(
            dinv[:, :, index], apply_block(upper_jac[:, :, index], value)
        )
        result[index] = value
    return jnp.stack(result, axis=1)


def solution(mesh):
    return jax.shard_map(
        body,
        mesh=mesh,
        in_specs=(
            P(None, "slab", "cross"),
            P(None, "slab", "cross"),
            P(None, None, "slab", "cross"),
            P(None, None, "slab", "cross"),
            P(None, None, "slab", "cross"),
            P(("slab", "cross"), None),
            P(("slab", "cross")),
            P(None, ("slab", "cross")),
            P(None, ("slab", "cross")),
            P(("slab", "cross"), None),
        ),
        out_specs=P(None, "slab", "cross"),
        check_vma=False,
    )
```

```python
import jax
import jax.numpy as jnp
from jax import lax
from jax.experimental import pallas as pl
from jax.experimental.pallas import tpu as pltpu
from jax.sharding import PartitionSpec as P


BLOCK_CELLS = 128


def apply_block(matrix, vector):
    return jnp.sum(matrix * vector[None], axis=1)


def chain_blocks(later, earlier):
    return jnp.sum(later[:, :, None] * earlier[None], axis=1)


def interpolate_at_owner(state_flat, request):
    width, resident = state_flat.shape
    blocks = resident // BLOCK_CELLS
    corners = request.shape[0] // 2
    wanted = request[:corners]
    wts = request[corners:]
    block = jnp.floor(wanted[0] * (1.0 / BLOCK_CELLS))
    lanes = lax.broadcasted_iota(jnp.float32, (BLOCK_CELLS, 1), 0)
    spread = jnp.zeros((BLOCK_CELLS, request.shape[1]), jnp.float32)
    for k in range(corners):
        offs = wanted[k] - block * BLOCK_CELLS
        spread = spread + jnp.where(offs[None, :] == lanes, wts[k][None, :], 0.0)
    table = state_flat.reshape(width, blocks, BLOCK_CELLS).transpose(1, 0, 2)
    table = table.reshape(blocks * width, BLOCK_CELLS)
    every = jnp.dot(table, spread, precision=lax.Precision.HIGH).reshape(blocks, width, -1)
    ids = lax.broadcasted_iota(jnp.float32, (blocks, 1, 1), 0)
    return jnp.sum(jnp.where(block[None, None, :] == ids, every, 0.0), axis=0)


def fold_kernel(index_ref, maps_ref, offsets_ref, out_ref, up_ref):
    peers = maps_ref.shape[0]
    width = out_ref.shape[1]
    square = width * width
    here = index_ref[0]
    zero = offsets_ref[0, 0] * 0.0

    def matvec(at, base, vector):
        rows = []
        for i in range(width):
            total = maps_ref[at, base + i * width] * vector[0]
            for j in range(1, width):
                total = total + maps_ref[at, base + i * width + j] * vector[j]
            rows.append(total)
        return rows

    def lower_step(at, carry):
        entry, kept = carry
        hit = at == here
        kept = tuple(jnp.where(hit, e, k) for e, k in zip(entry, kept))
        response = matvec(at, 2 * square, entry)
        for i in range(width):
            up_ref[at, i] = offsets_ref[at, width + i] + response[i]
        moved = matvec(at, 0, entry)
        entry = tuple(moved[i] + offsets_ref[at, i] for i in range(width))
        return entry, kept

    start = (tuple([zero] * width), tuple([zero] * width))
    _, low = lax.fori_loop(0, peers, lower_step, start)

    def upper_step(step, carry):
        at = peers - 1 - step
        entry, kept = carry
        hit = at == here
        kept = tuple(jnp.where(hit, e, k) for e, k in zip(entry, kept))
        moved = matvec(at, square, entry)
        entry = tuple(moved[i] + up_ref[at, i] for i in range(width))
        return entry, kept

    _, up = lax.fori_loop(0, peers, upper_step, start)
    for i in range(width):
        out_ref[0, i] = low[i]
        out_ref[1, i] = up[i]


def fold_entries(index, all_maps, every):
    peers, _, sub, lanes = all_maps.shape
    width = every.shape[1] // 2
    vmem = pltpu.MemorySpace.VMEM
    return pl.pallas_call(
        fold_kernel,
        out_shape=jax.ShapeDtypeStruct((2, width, sub, lanes), jnp.float32),
        in_specs=[
            pl.BlockSpec(memory_space=pltpu.MemorySpace.SMEM),
            pl.BlockSpec(memory_space=vmem),
            pl.BlockSpec(memory_space=vmem),
        ],
        out_specs=pl.BlockSpec(memory_space=vmem),
        scratch_shapes=[pltpu.VMEM((peers, width, sub, lanes), jnp.float32)],
        compiler_params=pltpu.CompilerParams(vmem_limit_bytes=48 * 1024 * 1024),
    )(index, all_maps, every)


def sweep_body(
    state, rhs, dinv, lower_jac, upper_jac, owner, donor_block, offsets, weights, receptor_perm
):
    width, planes, cells = state.shape
    resident_cells = planes * cells
    state_flat = state.reshape(width, resident_cells)
    devices = lax.axis_size(("slab", "cross"))
    slab_index = lax.axis_index("slab")
    fringe_rows = owner.shape[0]
    capacity = 4 * fringe_rows // devices
    blocks = resident_cells // BLOCK_CELLS
    square = width * width

    partial = []
    transfer = None
    for index in range(planes):
        step = chain_blocks(dinv[:, :, index], lower_jac[:, :, index])
        transfer = step if transfer is None else chain_blocks(step, transfer)
        partial.append(transfer)
    low_map = transfer
    up_steps = [chain_blocks(dinv[:, :, index], upper_jac[:, :, index]) for index in range(planes)]
    up_map = None
    response = partial[planes - 1]
    for index in range(planes - 1, -1, -1):
        up_map = up_steps[index] if up_map is None else chain_blocks(up_steps[index], up_map)
        if index < planes - 1:
            response = partial[index] + chain_blocks(up_steps[index], response)
    tile = (cells // BLOCK_CELLS, BLOCK_CELLS)
    maps = jnp.concatenate(
        [m.reshape((square,) + tile) for m in (low_map, up_map, response)], axis=0
    )
    all_maps = lax.all_gather(maps, "slab")
    peers = all_maps.shape[0]

    target = owner[:, 0]
    onehot = (target[:, None] == jnp.arange(devices, dtype=jnp.int32)[None, :]).astype(jnp.int32)
    slot = jnp.sum(jnp.cumsum(onehot, axis=0) * onehot, axis=1) - 1
    flat_slot = target * capacity + slot
    cells_wanted = donor_block[None, :] * BLOCK_CELLS + offsets
    payload = jnp.concatenate([cells_wanted.astype(jnp.float32), weights], axis=0)
    request = jnp.zeros((payload.shape[0], devices * capacity), jnp.float32)
    request = request.at[:, flat_slot].set(payload).reshape(-1, devices, capacity)
    received = lax.all_to_all(request, ("slab", "cross"), split_axis=1, concat_axis=1, tiled=True)
    answer = interpolate_at_owner(state_flat, received.reshape(received.shape[0], -1))
    answer = answer.reshape(width, devices, capacity)
    arrived = lax.all_to_all(answer, ("slab", "cross"), split_axis=1, concat_axis=1, tiled=True)
    interp = jnp.take(arrived.reshape(width, devices * capacity), flat_slot, axis=1)

    fringe_blocks = fringe_rows // BLOCK_CELLS
    chosen = receptor_perm[0, :fringe_blocks]
    hits = chosen[None, :] == jnp.arange(blocks, dtype=jnp.int32)[:, None]
    interp_blocks = interp.reshape(width, fringe_blocks, BLOCK_CELLS)
    placed = jnp.sum(
        jnp.where(hits[None, :, :, None], interp_blocks[:, None, :, :], 0.0), axis=2
    )
    state_blocks = state_flat.reshape(width, blocks, BLOCK_CELLS)
    rhs_blocks = rhs.reshape(width, blocks, BLOCK_CELLS)
    is_fringe = jnp.any(hits, axis=1)[None, :, None]
    forcing = jnp.where(is_fringe, placed - state_blocks, rhs_blocks)
    forcing = forcing.reshape(width, planes, cells)

    zero_lower = []
    value = jnp.zeros((width, cells), jnp.float32)
    for index in range(planes):
        value = apply_block(
            dinv[:, :, index], forcing[:, index] + apply_block(lower_jac[:, :, index], value)
        )
        zero_lower.append(value)
    value = jnp.zeros((width, cells), jnp.float32)
    for index in range(planes - 1, -1, -1):
        value = zero_lower[index] + apply_block(
            dinv[:, :, index], apply_block(upper_jac[:, :, index], value)
        )
    offsets_here = jnp.stack([zero_lower[planes - 1], value]).reshape((2, width) + tile)
    spread = jnp.broadcast_to(offsets_here[None], (peers,) + offsets_here.shape)
    every = lax.all_to_all(spread, "slab", 0, 0, tiled=True)

    every = every.reshape((peers, 2 * width) + tile)
    index = jnp.reshape(slab_index, (1,)).astype(jnp.int32)
    entries = fold_entries(index, all_maps, every).reshape(2, width, cells)
    low_entry = entries[0]
    up_entry = entries[1]

    lower_planes = []
    value = low_entry
    for index in range(planes):
        value = apply_block(
            dinv[:, :, index], forcing[:, index] + apply_block(lower_jac[:, :, index], value)
        )
        lower_planes.append(value)
    result = [None] * planes
    value = up_entry
    for index in range(planes - 1, -1, -1):
        value = lower_planes[index] + apply_block(
            dinv[:, :, index], apply_block(upper_jac[:, :, index], value)
        )
        result[index] = value
    return jnp.stack(result, axis=1)


def solution(mesh):
    return jax.shard_map(
        sweep_body,
        mesh=mesh,
        in_specs=(
            P(None, "slab", "cross"),
            P(None, "slab", "cross"),
            P(None, None, "slab", "cross"),
            P(None, None, "slab", "cross"),
            P(None, None, "slab", "cross"),
            P(("slab", "cross"), None),
            P(("slab", "cross")),
            P(None, ("slab", "cross")),
            P(None, ("slab", "cross")),
            P(("slab", "cross"), None),
        ),
        out_specs=P(None, "slab", "cross"),
        check_vma=False,
    )
```

```python
import jax
import jax.numpy as jnp
from jax import lax
from jax.experimental import pallas as pl
from jax.experimental.pallas import tpu as pltpu
from jax.sharding import PartitionSpec as P

BLOCK_CELLS = 128


def apply_block(matrix, vector):
    return jnp.sum(matrix * vector[None], axis=1)


def chain_blocks(later, earlier):
    return jnp.sum(later[:, :, None] * earlier[None], axis=1)


def interpolate_at_owner(state_flat, request):
    width, resident = state_flat.shape
    blocks = resident // BLOCK_CELLS
    corners = request.shape[0] // 2
    wanted = request[:corners]
    wts = request[corners:]
    block = jnp.floor(wanted[0] * (1.0 / BLOCK_CELLS))
    lanes = lax.broadcasted_iota(jnp.float32, (BLOCK_CELLS, 1), 0)
    spread = jnp.zeros((BLOCK_CELLS, request.shape[1]), jnp.float32)
    for k in range(corners):
        offs = wanted[k] - block * BLOCK_CELLS
        spread = spread + jnp.where(offs[None, :] == lanes, wts[k][None, :], 0.0)
    rows = 8
    table = state_flat.reshape(width, blocks, BLOCK_CELLS).transpose(1, 0, 2)
    table = jnp.pad(table, ((0, 0), (0, rows - width), (0, 0))).reshape(blocks * rows, BLOCK_CELLS)
    every = jnp.dot(table, spread, precision=lax.Precision.HIGH).reshape(blocks, rows, -1)
    ids = lax.broadcasted_iota(jnp.float32, (blocks, 1, 1), 0)
    return jnp.sum(jnp.where(block[None, None, :] == ids, every, 0.0), axis=0)[:width]


def fold_kernel(index_ref, maps_ref, offsets_ref, out_ref, up_ref):
    peers = maps_ref.shape[0]
    width = out_ref.shape[1]
    square = width * width
    here = index_ref[0]
    zero = offsets_ref[0, 0] * 0.0

    def matvec(at, base, vector):
        rows = []
        for i in range(width):
            total = maps_ref[at, base + i * width] * vector[0]
            for j in range(1, width):
                total = total + maps_ref[at, base + i * width + j] * vector[j]
            rows.append(total)
        return rows

    def lower_step(at, carry):
        entry, kept = carry
        hit = at == here
        kept = tuple(jnp.where(hit, e, k) for e, k in zip(entry, kept))
        response = matvec(at, 2 * square, entry)
        for i in range(width):
            up_ref[at, i] = offsets_ref[at, width + i] + response[i]
        moved = matvec(at, 0, entry)
        entry = tuple(moved[i] + offsets_ref[at, i] for i in range(width))
        return entry, kept

    start = (tuple([zero] * width), tuple([zero] * width))
    _, low = lax.fori_loop(0, peers, lower_step, start)

    def upper_step(step, carry):
        at = peers - 1 - step
        entry, kept = carry
        hit = at == here
        kept = tuple(jnp.where(hit, e, k) for e, k in zip(entry, kept))
        moved = matvec(at, square, entry)
        entry = tuple(moved[i] + up_ref[at, i] for i in range(width))
        return entry, kept

    _, up = lax.fori_loop(0, peers, upper_step, start)
    for i in range(width):
        out_ref[0, i] = low[i]
        out_ref[1, i] = up[i]


def fold_entries(index, all_maps, every):
    peers, _, sub, lanes = all_maps.shape
    width = every.shape[1] // 2
    vmem = pltpu.MemorySpace.VMEM
    return pl.pallas_call(
        fold_kernel,
        out_shape=jax.ShapeDtypeStruct((2, width, sub, lanes), jnp.float32),
        in_specs=[
            pl.BlockSpec(memory_space=pltpu.MemorySpace.SMEM),
            pl.BlockSpec(memory_space=vmem),
            pl.BlockSpec(memory_space=vmem),
        ],
        out_specs=pl.BlockSpec(memory_space=vmem),
        scratch_shapes=[pltpu.VMEM((peers, width, sub, lanes), jnp.float32)],
        compiler_params=pltpu.CompilerParams(vmem_limit_bytes=48 * 1024 * 1024),
    )(index, all_maps, every)


def sweep_body(
    state, rhs, dinv, lower_jac, upper_jac, owner, donor_block, offsets, weights, receptor_perm
):
    width, planes, cells = state.shape
    resident_cells = planes * cells
    state_flat = state.reshape(width, resident_cells)
    devices = lax.axis_size(("slab", "cross"))
    slab_index = lax.axis_index("slab")
    fringe_rows = owner.shape[0]
    capacity = 4 * fringe_rows // devices
    blocks = resident_cells // BLOCK_CELLS
    square = width * width

    partial = []
    transfer = None
    for index in range(planes):
        step = chain_blocks(dinv[:, :, index], lower_jac[:, :, index])
        transfer = step if transfer is None else chain_blocks(step, transfer)
        partial.append(transfer)
    low_map = transfer
    up_steps = [chain_blocks(dinv[:, :, index], upper_jac[:, :, index]) for index in range(planes)]
    up_map = None
    response = partial[planes - 1]
    for index in range(planes - 1, -1, -1):
        up_map = up_steps[index] if up_map is None else chain_blocks(up_steps[index], up_map)
        if index < planes - 1:
            response = partial[index] + chain_blocks(up_steps[index], response)
    tile = (cells // BLOCK_CELLS, BLOCK_CELLS)
    maps = jnp.concatenate(
        [m.reshape((square,) + tile) for m in (low_map, up_map, response)], axis=0
    )
    all_maps = lax.all_gather(maps, "slab")
    peers = all_maps.shape[0]

    target = owner[:, 0]
    onehot = (target[:, None] == jnp.arange(devices, dtype=jnp.int32)[None, :]).astype(jnp.int32)
    slot = jnp.sum(jnp.cumsum(onehot, axis=0) * onehot, axis=1) - 1
    flat_slot = target * capacity + slot
    cells_wanted = donor_block[None, :] * BLOCK_CELLS + offsets
    payload = jnp.concatenate([cells_wanted.astype(jnp.float32), weights], axis=0)
    request = jnp.zeros((payload.shape[0], devices * capacity), jnp.float32)
    request = request.at[:, flat_slot].set(payload).reshape(-1, devices, capacity)
    received = lax.all_to_all(request, ("slab", "cross"), split_axis=1, concat_axis=1, tiled=True)
    answer = interpolate_at_owner(state_flat, received.reshape(received.shape[0], -1))
    answer = answer.reshape(width, devices, capacity)
    arrived = lax.all_to_all(answer, ("slab", "cross"), split_axis=1, concat_axis=1, tiled=True)
    interp = jnp.take(arrived.reshape(width, devices * capacity), flat_slot, axis=1)

    fringe_blocks = fringe_rows // BLOCK_CELLS
    chosen = receptor_perm[0, :fringe_blocks]
    hits = chosen[None, :] == jnp.arange(blocks, dtype=jnp.int32)[:, None]
    interp_blocks = interp.reshape(width, fringe_blocks, BLOCK_CELLS)
    placed = jnp.sum(
        jnp.where(hits[None, :, :, None], interp_blocks[:, None, :, :], 0.0), axis=2
    )
    state_blocks = state_flat.reshape(width, blocks, BLOCK_CELLS)
    rhs_blocks = rhs.reshape(width, blocks, BLOCK_CELLS)
    is_fringe = jnp.any(hits, axis=1)[None, :, None]
    forcing = jnp.where(is_fringe, placed - state_blocks, rhs_blocks)
    forcing = forcing.reshape(width, planes, cells)

    zero_lower = []
    value = jnp.zeros((width, cells), jnp.float32)
    for index in range(planes):
        value = apply_block(
            dinv[:, :, index], forcing[:, index] + apply_block(lower_jac[:, :, index], value)
        )
        zero_lower.append(value)
    value = jnp.zeros((width, cells), jnp.float32)
    for index in range(planes - 1, -1, -1):
        value = zero_lower[index] + apply_block(
            dinv[:, :, index], apply_block(upper_jac[:, :, index], value)
        )
    offsets_here = jnp.stack([zero_lower[planes - 1], value]).reshape((2, width) + tile)
    spread = jnp.broadcast_to(offsets_here[None], (peers,) + offsets_here.shape)
    every = lax.all_to_all(spread, "slab", 0, 0, tiled=True)

    every = every.reshape((peers, 2 * width) + tile)
    index = jnp.reshape(slab_index, (1,)).astype(jnp.int32)
    entries = fold_entries(index, all_maps, every).reshape(2, width, cells)
    low_entry = entries[0]
    up_entry = entries[1]

    lower_planes = []
    value = low_entry
    for index in range(planes):
        value = apply_block(
            dinv[:, :, index], forcing[:, index] + apply_block(lower_jac[:, :, index], value)
        )
        lower_planes.append(value)
    result = [None] * planes
    value = up_entry
    for index in range(planes - 1, -1, -1):
        value = lower_planes[index] + apply_block(
            dinv[:, :, index], apply_block(upper_jac[:, :, index], value)
        )
        result[index] = value
    return jnp.stack(result, axis=1)


def solution(mesh):
    return jax.shard_map(
        sweep_body,
        mesh=mesh,
        in_specs=(
            P(None, "slab", "cross"),
            P(None, "slab", "cross"),
            P(None, None, "slab", "cross"),
            P(None, None, "slab", "cross"),
            P(None, None, "slab", "cross"),
            P(("slab", "cross"), None),
            P(("slab", "cross")),
            P(None, ("slab", "cross")),
            P(None, ("slab", "cross")),
            P(("slab", "cross"), None),
        ),
        out_specs=P(None, "slab", "cross"),
        check_vma=False,
    )
```

```python
import jax
import jax.numpy as jnp
from jax import lax
from jax.experimental import pallas as pl
from jax.experimental.pallas import tpu as pltpu
from jax.sharding import PartitionSpec as P

BLOCK_CELLS = 128
HIGHEST = lax.Precision.HIGHEST


def apply_block(matrix, vector):
    return jnp.sum(matrix * vector[None], axis=1)


def chain_blocks(later, earlier):
    return jnp.sum(later[:, :, None] * earlier[None], axis=1)


def owner_kernel(request_ref, table_ref, out_ref):
    corners = request_ref.shape[0] // 2
    rows = out_ref.shape[0]
    blocks = table_ref.shape[0] // rows
    chunk = 512
    table = table_ref[...]
    lanes = lax.broadcasted_iota(jnp.int32, (BLOCK_CELLS, chunk), 0).astype(jnp.float32)
    for part in range(request_ref.shape[1] // chunk):
        window = pl.ds(part * chunk, chunk)
        wanted = request_ref[0:corners, window]
        wts = request_ref[corners : 2 * corners, window]
        block = jnp.floor(wanted[0:1] * (1.0 / BLOCK_CELLS))
        spread = jnp.where(wanted[0:1] - block * BLOCK_CELLS == lanes, wts[0:1], 0.0)
        for k in range(1, corners):
            offs = wanted[k : k + 1] - block * BLOCK_CELLS
            spread = spread + jnp.where(offs == lanes, wts[k : k + 1], 0.0)
        every = jnp.dot(table, spread, precision=HIGHEST, preferred_element_type=jnp.float32)
        total = jnp.where(block == 0.0, every[0:rows], 0.0)
        for at in range(1, blocks):
            total = total + jnp.where(block == float(at), every[at * rows : (at + 1) * rows], 0.0)
        out_ref[:, window] = total


def interpolate_at_owner(state_flat, request):
    width, resident = state_flat.shape
    blocks = resident // BLOCK_CELLS
    rows = 8
    table = state_flat.reshape(width, blocks, BLOCK_CELLS).transpose(1, 0, 2)
    table = jnp.pad(table, ((0, 0), (0, rows - width), (0, 0))).reshape(blocks * rows, BLOCK_CELLS)
    vmem = pltpu.MemorySpace.VMEM
    out = pl.pallas_call(
        owner_kernel,
        out_shape=jax.ShapeDtypeStruct((rows, request.shape[1]), jnp.float32),
        in_specs=[pl.BlockSpec(memory_space=vmem), pl.BlockSpec(memory_space=vmem)],
        out_specs=pl.BlockSpec(memory_space=vmem),
    )(request, table)
    return out[:width]


def fold_kernel(index_ref, maps_ref, offsets_ref, out_ref, up_ref):
    peers = maps_ref.shape[0]
    width = out_ref.shape[1]
    square = width * width
    here = index_ref[0]
    zero = offsets_ref[0, 0] * 0.0

    def matvec(at, base, vector):
        rows = []
        for i in range(width):
            total = maps_ref[at, base + i * width] * vector[0]
            for j in range(1, width):
                total = total + maps_ref[at, base + i * width + j] * vector[j]
            rows.append(total)
        return rows

    def lower_step(at, carry):
        entry, kept = carry
        hit = at == here
        kept = tuple(jnp.where(hit, e, k) for e, k in zip(entry, kept))
        response = matvec(at, 2 * square, entry)
        for i in range(width):
            up_ref[at, i] = offsets_ref[at, width + i] + response[i]
        moved = matvec(at, 0, entry)
        entry = tuple(moved[i] + offsets_ref[at, i] for i in range(width))
        return entry, kept

    start = (tuple([zero] * width), tuple([zero] * width))
    _, low = lax.fori_loop(0, peers, lower_step, start)

    def upper_step(step, carry):
        at = peers - 1 - step
        entry, kept = carry
        hit = at == here
        kept = tuple(jnp.where(hit, e, k) for e, k in zip(entry, kept))
        moved = matvec(at, square, entry)
        entry = tuple(moved[i] + up_ref[at, i] for i in range(width))
        return entry, kept

    _, up = lax.fori_loop(0, peers, upper_step, start)
    for i in range(width):
        out_ref[0, i] = low[i]
        out_ref[1, i] = up[i]


def fold_entries(index, all_maps, every):
    peers, _, sub, lanes = all_maps.shape
    width = every.shape[1] // 2
    vmem = pltpu.MemorySpace.VMEM
    return pl.pallas_call(
        fold_kernel,
        out_shape=jax.ShapeDtypeStruct((2, width, sub, lanes), jnp.float32),
        in_specs=[
            pl.BlockSpec(memory_space=pltpu.MemorySpace.SMEM),
            pl.BlockSpec(memory_space=vmem),
            pl.BlockSpec(memory_space=vmem),
        ],
        out_specs=pl.BlockSpec(memory_space=vmem),
        scratch_shapes=[pltpu.VMEM((peers, width, sub, lanes), jnp.float32)],
        compiler_params=pltpu.CompilerParams(vmem_limit_bytes=48 * 1024 * 1024),
    )(index, all_maps, every)


def sweep_body(
    state, rhs, dinv, lower_jac, upper_jac, owner, donor_block, offsets, weights, receptor_perm
):
    width, planes, cells = state.shape
    resident_cells = planes * cells
    state_flat = state.reshape(width, resident_cells)
    devices = lax.axis_size(("slab", "cross"))
    slab_index = lax.axis_index("slab")
    fringe_rows = owner.shape[0]
    capacity = 4 * fringe_rows // devices
    blocks = resident_cells // BLOCK_CELLS
    square = width * width

    partial = []
    transfer = None
    for index in range(planes):
        step = chain_blocks(dinv[:, :, index], lower_jac[:, :, index])
        transfer = step if transfer is None else chain_blocks(step, transfer)
        partial.append(transfer)
    low_map = transfer
    up_steps = [chain_blocks(dinv[:, :, index], upper_jac[:, :, index]) for index in range(planes)]
    up_map = None
    response = partial[planes - 1]
    for index in range(planes - 1, -1, -1):
        up_map = up_steps[index] if up_map is None else chain_blocks(up_steps[index], up_map)
        if index < planes - 1:
            response = partial[index] + chain_blocks(up_steps[index], response)
    tile = (cells // BLOCK_CELLS, BLOCK_CELLS)
    maps = jnp.concatenate(
        [m.reshape((square,) + tile) for m in (low_map, up_map, response)], axis=0
    )
    all_maps = lax.all_gather(maps, "slab")
    peers = all_maps.shape[0]

    target = owner[:, 0]
    onehot = (target[:, None] == jnp.arange(devices, dtype=jnp.int32)[None, :]).astype(jnp.int32)
    slot = jnp.sum(jnp.cumsum(onehot, axis=0) * onehot, axis=1) - 1
    flat_slot = target * capacity + slot
    cells_wanted = donor_block[None, :] * BLOCK_CELLS + offsets
    payload = jnp.concatenate([cells_wanted.astype(jnp.float32), weights], axis=0)
    request = jnp.zeros((payload.shape[0], devices * capacity), jnp.float32)
    request = request.at[:, flat_slot].set(payload).reshape(-1, devices, capacity)
    received = lax.all_to_all(request, ("slab", "cross"), split_axis=1, concat_axis=1, tiled=True)
    answer = interpolate_at_owner(state_flat, received.reshape(received.shape[0], -1))
    answer = answer.reshape(width, devices, capacity)
    arrived = lax.all_to_all(answer, ("slab", "cross"), split_axis=1, concat_axis=1, tiled=True)
    interp = jnp.take(arrived.reshape(width, devices * capacity), flat_slot, axis=1)

    fringe_blocks = fringe_rows // BLOCK_CELLS
    chosen = receptor_perm[0, :fringe_blocks]
    hits = chosen[None, :] == jnp.arange(blocks, dtype=jnp.int32)[:, None]
    interp_blocks = interp.reshape(width, fringe_blocks, BLOCK_CELLS)
    placed = jnp.sum(
        jnp.where(hits[None, :, :, None], interp_blocks[:, None, :, :], 0.0), axis=2
    )
    state_blocks = state_flat.reshape(width, blocks, BLOCK_CELLS)
    rhs_blocks = rhs.reshape(width, blocks, BLOCK_CELLS)
    is_fringe = jnp.any(hits, axis=1)[None, :, None]
    forcing = jnp.where(is_fringe, placed - state_blocks, rhs_blocks)
    forcing = forcing.reshape(width, planes, cells)

    zero_lower = []
    value = jnp.zeros((width, cells), jnp.float32)
    for index in range(planes):
        value = apply_block(
            dinv[:, :, index], forcing[:, index] + apply_block(lower_jac[:, :, index], value)
        )
        zero_lower.append(value)
    value = jnp.zeros((width, cells), jnp.float32)
    for index in range(planes - 1, -1, -1):
        value = zero_lower[index] + apply_block(
            dinv[:, :, index], apply_block(upper_jac[:, :, index], value)
        )
    offsets_here = jnp.stack([zero_lower[planes - 1], value]).reshape((2, width) + tile)
    spread = jnp.broadcast_to(offsets_here[None], (peers,) + offsets_here.shape)
    every = lax.all_to_all(spread, "slab", 0, 0, tiled=True)

    every = every.reshape((peers, 2 * width) + tile)
    index = jnp.reshape(slab_index, (1,)).astype(jnp.int32)
    entries = fold_entries(index, all_maps, every).reshape(2, width, cells)
    low_entry = entries[0]
    up_entry = entries[1]

    lower_planes = []
    value = low_entry
    for index in range(planes):
        value = apply_block(
            dinv[:, :, index], forcing[:, index] + apply_block(lower_jac[:, :, index], value)
        )
        lower_planes.append(value)
    result = [None] * planes
    value = up_entry
    for index in range(planes - 1, -1, -1):
        value = lower_planes[index] + apply_block(
            dinv[:, :, index], apply_block(upper_jac[:, :, index], value)
        )
        result[index] = value
    return jnp.stack(result, axis=1)


def solution(mesh):
    return jax.shard_map(
        sweep_body,
        mesh=mesh,
        in_specs=(
            P(None, "slab", "cross"),
            P(None, "slab", "cross"),
            P(None, None, "slab", "cross"),
            P(None, None, "slab", "cross"),
            P(None, None, "slab", "cross"),
            P(("slab", "cross"), None),
            P(("slab", "cross")),
            P(None, ("slab", "cross")),
            P(None, ("slab", "cross")),
            P(("slab", "cross"), None),
        ),
        out_specs=P(None, "slab", "cross"),
        check_vma=False,
    )
```

```python
import jax
import jax.numpy as jnp
from jax import lax
from jax.experimental import pallas as pl
from jax.experimental.pallas import tpu as pltpu
from jax.sharding import PartitionSpec as P

BLOCK_CELLS = 128
HIGHEST = lax.Precision.HIGHEST


def apply_block(matrix, vector):
    return jnp.sum(matrix * vector[None], axis=1)


def chain_blocks(later, earlier):
    return jnp.sum(later[:, :, None] * earlier[None], axis=1)


def owner_kernel(request_ref, table_ref, out_ref):
    corners = request_ref.shape[0] // 2
    rows = out_ref.shape[0]
    blocks = table_ref.shape[0] // rows
    chunk = 512
    table = table_ref[...]
    lanes = lax.broadcasted_iota(jnp.int32, (BLOCK_CELLS, chunk), 0).astype(jnp.float32)
    for part in range(request_ref.shape[1] // chunk):
        window = pl.ds(part * chunk, chunk)
        wanted = request_ref[0:corners, window]
        wts = request_ref[corners : 2 * corners, window]
        block = jnp.floor(wanted[0:1] * (1.0 / BLOCK_CELLS))
        spread = jnp.where(wanted[0:1] - block * BLOCK_CELLS == lanes, wts[0:1], 0.0)
        for k in range(1, corners):
            offs = wanted[k : k + 1] - block * BLOCK_CELLS
            spread = spread + jnp.where(offs == lanes, wts[k : k + 1], 0.0)
        every = jnp.dot(table, spread, precision=HIGHEST, preferred_element_type=jnp.float32)
        total = jnp.where(block == 0.0, every[0:rows], 0.0)
        for at in range(1, blocks):
            total = total + jnp.where(block == float(at), every[at * rows : (at + 1) * rows], 0.0)
        out_ref[:, window] = total


def interpolate_at_owner(state_flat, request):
    width, resident = state_flat.shape
    blocks = resident // BLOCK_CELLS
    rows = 8
    table = state_flat.reshape(width, blocks, BLOCK_CELLS).transpose(1, 0, 2)
    table = jnp.pad(table, ((0, 0), (0, rows - width), (0, 0))).reshape(blocks * rows, BLOCK_CELLS)
    vmem = pltpu.MemorySpace.VMEM
    out = pl.pallas_call(
        owner_kernel,
        out_shape=jax.ShapeDtypeStruct((rows, request.shape[1]), jnp.float32),
        in_specs=[pl.BlockSpec(memory_space=vmem), pl.BlockSpec(memory_space=vmem)],
        out_specs=pl.BlockSpec(memory_space=vmem),
    )(request, table)
    return out[:width]


def fold_kernel(index_ref, maps_hbm, offsets_ref, out_ref, up_ref, maps_ref, arrived):
    peers = maps_ref.shape[0]
    width = out_ref.shape[1]
    square = width * width
    here = index_ref[0]
    zero = offsets_ref[0, 0] * 0.0

    def copy(at):
        return pltpu.make_async_copy(maps_hbm.at[at], maps_ref.at[at], arrived.at[at])

    for at in range(peers):
        copy(at).start()

    def matvec(at, base, vector):
        rows = []
        for i in range(width):
            total = maps_ref[at, base + i * width] * vector[0]
            for j in range(1, width):
                total = total + maps_ref[at, base + i * width + j] * vector[j]
            rows.append(total)
        return rows

    def lower_step(at, carry):
        copy(at).wait()
        entry, kept = carry
        hit = at == here
        kept = tuple(jnp.where(hit, e, k) for e, k in zip(entry, kept))
        response = matvec(at, 2 * square, entry)
        for i in range(width):
            up_ref[at, i] = offsets_ref[at, width + i] + response[i]
        moved = matvec(at, 0, entry)
        entry = tuple(moved[i] + offsets_ref[at, i] for i in range(width))
        return entry, kept

    start = (tuple([zero] * width), tuple([zero] * width))
    _, low = lax.fori_loop(0, peers, lower_step, start, unroll=True)

    def upper_step(step, carry):
        at = peers - 1 - step
        entry, kept = carry
        hit = at == here
        kept = tuple(jnp.where(hit, e, k) for e, k in zip(entry, kept))
        moved = matvec(at, square, entry)
        entry = tuple(moved[i] + up_ref[at, i] for i in range(width))
        return entry, kept

    _, up = lax.fori_loop(0, peers, upper_step, start, unroll=True)
    for i in range(width):
        out_ref[0, i] = low[i]
        out_ref[1, i] = up[i]


def fold_entries(index, all_maps, every):
    peers, _, sub, lanes = all_maps.shape
    width = every.shape[1] // 2
    vmem = pltpu.MemorySpace.VMEM
    return pl.pallas_call(
        fold_kernel,
        out_shape=jax.ShapeDtypeStruct((2, width, sub, lanes), jnp.float32),
        in_specs=[
            pl.BlockSpec(memory_space=pltpu.MemorySpace.SMEM),
            pl.BlockSpec(memory_space=pl.ANY),
            pl.BlockSpec(memory_space=vmem),
        ],
        out_specs=pl.BlockSpec(memory_space=vmem),
        scratch_shapes=[
            pltpu.VMEM((peers, width, sub, lanes), jnp.float32),
            pltpu.VMEM(all_maps.shape, jnp.float32),
            pltpu.SemaphoreType.DMA((peers,)),
        ],
        compiler_params=pltpu.CompilerParams(vmem_limit_bytes=48 * 1024 * 1024),
    )(index, all_maps, every)


def sweep_body(
    state, rhs, dinv, lower_jac, upper_jac, owner, donor_block, offsets, weights, receptor_perm
):
    width, planes, cells = state.shape
    resident_cells = planes * cells
    state_flat = state.reshape(width, resident_cells)
    devices = lax.axis_size(("slab", "cross"))
    slab_index = lax.axis_index("slab")
    fringe_rows = owner.shape[0]
    capacity = 4 * fringe_rows // devices
    blocks = resident_cells // BLOCK_CELLS
    square = width * width

    partial = []
    transfer = None
    for index in range(planes):
        step = chain_blocks(dinv[:, :, index], lower_jac[:, :, index])
        transfer = step if transfer is None else chain_blocks(step, transfer)
        partial.append(transfer)
    low_map = transfer
    up_steps = [chain_blocks(dinv[:, :, index], upper_jac[:, :, index]) for index in range(planes)]
    up_map = None
    response = partial[planes - 1]
    for index in range(planes - 1, -1, -1):
        up_map = up_steps[index] if up_map is None else chain_blocks(up_steps[index], up_map)
        if index < planes - 1:
            response = partial[index] + chain_blocks(up_steps[index], response)
    tile = (cells // BLOCK_CELLS, BLOCK_CELLS)
    maps = jnp.concatenate(
        [m.reshape((square,) + tile) for m in (low_map, up_map, response)], axis=0
    )
    all_maps = lax.all_gather(maps, "slab")
    peers = all_maps.shape[0]

    target = owner[:, 0]
    onehot = (target[:, None] == jnp.arange(devices, dtype=jnp.int32)[None, :]).astype(jnp.int32)
    slot = jnp.sum(jnp.cumsum(onehot, axis=0) * onehot, axis=1) - 1
    flat_slot = target * capacity + slot
    cells_wanted = donor_block[None, :] * BLOCK_CELLS + offsets
    payload = jnp.concatenate([cells_wanted.astype(jnp.float32), weights], axis=0)
    request = jnp.zeros((payload.shape[0], devices * capacity), jnp.float32)
    request = request.at[:, flat_slot].set(payload).reshape(-1, devices, capacity)
    received = lax.all_to_all(request, ("slab", "cross"), split_axis=1, concat_axis=1, tiled=True)
    answer = interpolate_at_owner(state_flat, received.reshape(received.shape[0], -1))
    answer = answer.reshape(width, devices, capacity)
    arrived = lax.all_to_all(answer, ("slab", "cross"), split_axis=1, concat_axis=1, tiled=True)
    interp = jnp.take(arrived.reshape(width, devices * capacity), flat_slot, axis=1)

    fringe_blocks = fringe_rows // BLOCK_CELLS
    chosen = receptor_perm[0, :fringe_blocks]
    hits = chosen[None, :] == jnp.arange(blocks, dtype=jnp.int32)[:, None]
    interp_blocks = interp.reshape(width, fringe_blocks, BLOCK_CELLS)
    placed = jnp.sum(
        jnp.where(hits[None, :, :, None], interp_blocks[:, None, :, :], 0.0), axis=2
    )
    state_blocks = state_flat.reshape(width, blocks, BLOCK_CELLS)
    rhs_blocks = rhs.reshape(width, blocks, BLOCK_CELLS)
    is_fringe = jnp.any(hits, axis=1)[None, :, None]
    forcing = jnp.where(is_fringe, placed - state_blocks, rhs_blocks)
    forcing = forcing.reshape(width, planes, cells)

    zero_lower = []
    value = jnp.zeros((width, cells), jnp.float32)
    for index in range(planes):
        value = apply_block(
            dinv[:, :, index], forcing[:, index] + apply_block(lower_jac[:, :, index], value)
        )
        zero_lower.append(value)
    value = jnp.zeros((width, cells), jnp.float32)
    for index in range(planes - 1, -1, -1):
        value = zero_lower[index] + apply_block(
            dinv[:, :, index], apply_block(upper_jac[:, :, index], value)
        )
    offsets_here = jnp.stack([zero_lower[planes - 1], value]).reshape((2, width) + tile)
    spread = jnp.broadcast_to(offsets_here[None], (peers,) + offsets_here.shape)
    every = lax.all_to_all(spread, "slab", 0, 0, tiled=True)

    every = every.reshape((peers, 2 * width) + tile)
    index = jnp.reshape(slab_index, (1,)).astype(jnp.int32)
    entries = fold_entries(index, all_maps, every).reshape(2, width, cells)
    low_entry = entries[0]
    up_entry = entries[1]

    lower_planes = []
    value = low_entry
    for index in range(planes):
        value = apply_block(
            dinv[:, :, index], forcing[:, index] + apply_block(lower_jac[:, :, index], value)
        )
        lower_planes.append(value)
    result = [None] * planes
    value = up_entry
    for index in range(planes - 1, -1, -1):
        value = lower_planes[index] + apply_block(
            dinv[:, :, index], apply_block(upper_jac[:, :, index], value)
        )
        result[index] = value
    return jnp.stack(result, axis=1)


def solution(mesh):
    return jax.shard_map(
        sweep_body,
        mesh=mesh,
        in_specs=(
            P(None, "slab", "cross"),
            P(None, "slab", "cross"),
            P(None, None, "slab", "cross"),
            P(None, None, "slab", "cross"),
            P(None, None, "slab", "cross"),
            P(("slab", "cross"), None),
            P(("slab", "cross")),
            P(None, ("slab", "cross")),
            P(None, ("slab", "cross")),
            P(("slab", "cross"), None),
        ),
        out_specs=P(None, "slab", "cross"),
        check_vma=False,
    )
```

```python
import jax
import jax.numpy as jnp
from jax import lax
from jax.experimental import pallas as pl
from jax.experimental.pallas import tpu as pltpu
from jax.sharding import PartitionSpec as P

BLOCK_CELLS = 128
HIGHEST = lax.Precision.HIGHEST


def apply_block(matrix, vector):
    return jnp.sum(matrix * vector[None], axis=1)


def chain_blocks(later, earlier):
    return jnp.sum(later[:, :, None] * earlier[None], axis=1)


def owner_kernel(request_ref, table_ref, out_ref):
    corners = request_ref.shape[0] // 2
    rows = out_ref.shape[0]
    blocks = table_ref.shape[0] // rows
    chunk = 512
    table = table_ref[...]
    lanes = lax.broadcasted_iota(jnp.int32, (BLOCK_CELLS, chunk), 0).astype(jnp.float32)
    for part in range(request_ref.shape[1] // chunk):
        window = pl.ds(part * chunk, chunk)
        wanted = request_ref[0:corners, window]
        wts = request_ref[corners : 2 * corners, window]
        block = jnp.floor(wanted[0:1] * (1.0 / BLOCK_CELLS))
        spread = jnp.where(wanted[0:1] - block * BLOCK_CELLS == lanes, wts[0:1], 0.0)
        for k in range(1, corners):
            offs = wanted[k : k + 1] - block * BLOCK_CELLS
            spread = spread + jnp.where(offs == lanes, wts[k : k + 1], 0.0)
        every = jnp.dot(table, spread, precision=HIGHEST, preferred_element_type=jnp.float32)
        total = jnp.where(block == 0.0, every[0:rows], 0.0)
        for at in range(1, blocks):
            total = total + jnp.where(block == float(at), every[at * rows : (at + 1) * rows], 0.0)
        out_ref[:, window] = total


def interpolate_at_owner(state_flat, request):
    width, resident = state_flat.shape
    blocks = resident // BLOCK_CELLS
    rows = 8
    table = state_flat.reshape(width, blocks, BLOCK_CELLS).transpose(1, 0, 2)
    table = jnp.pad(table, ((0, 0), (0, rows - width), (0, 0))).reshape(blocks * rows, BLOCK_CELLS)
    vmem = pltpu.MemorySpace.VMEM
    out = pl.pallas_call(
        owner_kernel,
        out_shape=jax.ShapeDtypeStruct((rows, request.shape[1]), jnp.float32),
        in_specs=[pl.BlockSpec(memory_space=vmem), pl.BlockSpec(memory_space=vmem)],
        out_specs=pl.BlockSpec(memory_space=vmem),
    )(request, table)
    return out[:width]


def fold_kernel(index_ref, maps_hbm, offsets_ref, out_ref, up_ref, maps_ref, arrived):
    peers = maps_ref.shape[0]
    width = out_ref.shape[1]
    square = width * width
    here = index_ref[0]
    zero = offsets_ref[0, 0] * 0.0

    def copy(at):
        return pltpu.make_async_copy(maps_hbm.at[at], maps_ref.at[at], arrived.at[at])

    for at in range(peers):
        copy(at).start()

    def matvec(at, base, vector):
        rows = []
        for i in range(width):
            total = maps_ref[at, base + i * width] * vector[0]
            for j in range(1, width):
                total = total + maps_ref[at, base + i * width + j] * vector[j]
            rows.append(total)
        return rows

    def lower_step(at, carry):
        copy(at).wait()
        entry, kept = carry
        hit = at == here
        kept = tuple(jnp.where(hit, e, k) for e, k in zip(entry, kept))
        response = matvec(at, 2 * square, entry)
        for i in range(width):
            up_ref[at, i] = offsets_ref[at, width + i] + response[i]
        moved = matvec(at, 0, entry)
        entry = tuple(moved[i] + offsets_ref[at, i] for i in range(width))
        return entry, kept

    start = (tuple([zero] * width), tuple([zero] * width))
    _, low = lax.fori_loop(0, peers, lower_step, start, unroll=True)

    def upper_step(step, carry):
        at = peers - 1 - step
        entry, kept = carry
        hit = at == here
        kept = tuple(jnp.where(hit, e, k) for e, k in zip(entry, kept))
        moved = matvec(at, square, entry)
        entry = tuple(moved[i] + up_ref[at, i] for i in range(width))
        return entry, kept

    _, up = lax.fori_loop(0, peers, upper_step, start, unroll=True)
    for i in range(width):
        out_ref[0, i] = low[i]
        out_ref[1, i] = up[i]


def fold_entries(index, all_maps, every):
    peers, _, sub, lanes = all_maps.shape
    width = every.shape[1] // 2
    vmem = pltpu.MemorySpace.VMEM
    return pl.pallas_call(
        fold_kernel,
        out_shape=jax.ShapeDtypeStruct((2, width, sub, lanes), jnp.float32),
        in_specs=[
            pl.BlockSpec(memory_space=pltpu.MemorySpace.SMEM),
            pl.BlockSpec(memory_space=pl.ANY),
            pl.BlockSpec(memory_space=vmem),
        ],
        out_specs=pl.BlockSpec(memory_space=vmem),
        scratch_shapes=[
            pltpu.VMEM((peers, width, sub, lanes), jnp.float32),
            pltpu.VMEM(all_maps.shape, jnp.float32),
            pltpu.SemaphoreType.DMA((peers,)),
        ],
        compiler_params=pltpu.CompilerParams(vmem_limit_bytes=48 * 1024 * 1024),
    )(index, all_maps, every)


def sweep_body(
    state, rhs, dinv, lower_jac, upper_jac, owner, donor_block, offsets, weights, receptor_perm
):
    width, planes, cells = state.shape
    resident_cells = planes * cells
    state_flat = state.reshape(width, resident_cells)
    devices = lax.axis_size(("slab", "cross"))
    slab_index = lax.axis_index("slab")
    fringe_rows = owner.shape[0]
    capacity = 4 * fringe_rows // devices
    blocks = resident_cells // BLOCK_CELLS
    square = width * width

    tile = (cells // BLOCK_CELLS, BLOCK_CELLS)
    tiled_dinv = dinv.reshape((width, width, planes) + tile)
    tiled_lower = lower_jac.reshape((width, width, planes) + tile)
    tiled_upper = upper_jac.reshape((width, width, planes) + tile)
    partial = []
    transfer = None
    for index in range(planes):
        step = chain_blocks(tiled_dinv[:, :, index], tiled_lower[:, :, index])
        transfer = step if transfer is None else chain_blocks(step, transfer)
        partial.append(transfer)
    low_map = transfer
    up_steps = [
        chain_blocks(tiled_dinv[:, :, index], tiled_upper[:, :, index])
        for index in range(planes)
    ]
    up_map = None
    response = partial[planes - 1]
    for index in range(planes - 1, -1, -1):
        up_map = up_steps[index] if up_map is None else chain_blocks(up_steps[index], up_map)
        if index < planes - 1:
            response = partial[index] + chain_blocks(up_steps[index], response)
    maps = jnp.concatenate(
        [m.reshape((square,) + tile) for m in (low_map, up_map, response)], axis=0
    )
    all_maps = lax.all_gather(maps, "slab")
    peers = all_maps.shape[0]

    target = owner[:, 0]
    onehot = (target[:, None] == jnp.arange(devices, dtype=jnp.int32)[None, :]).astype(jnp.int32)
    slot = jnp.sum(jnp.cumsum(onehot, axis=0) * onehot, axis=1) - 1
    flat_slot = target * capacity + slot
    cells_wanted = donor_block[None, :] * BLOCK_CELLS + offsets
    payload = jnp.concatenate([cells_wanted.astype(jnp.float32), weights], axis=0)
    request = jnp.zeros((payload.shape[0], devices * capacity), jnp.float32)
    request = request.at[:, flat_slot].set(payload).reshape(-1, devices, capacity)
    received = lax.all_to_all(request, ("slab", "cross"), split_axis=1, concat_axis=1, tiled=True)
    answer = interpolate_at_owner(state_flat, received.reshape(received.shape[0], -1))
    answer = answer.reshape(width, devices, capacity)
    arrived = lax.all_to_all(answer, ("slab", "cross"), split_axis=1, concat_axis=1, tiled=True)
    interp = jnp.take(arrived.reshape(width, devices * capacity), flat_slot, axis=1)

    fringe_blocks = fringe_rows // BLOCK_CELLS
    chosen = receptor_perm[0, :fringe_blocks]
    hits = chosen[None, :] == jnp.arange(blocks, dtype=jnp.int32)[:, None]
    interp_blocks = interp.reshape(width, fringe_blocks, BLOCK_CELLS)
    placed = jnp.sum(
        jnp.where(hits[None, :, :, None], interp_blocks[:, None, :, :], 0.0), axis=2
    )
    state_blocks = state_flat.reshape(width, blocks, BLOCK_CELLS)
    rhs_blocks = rhs.reshape(width, blocks, BLOCK_CELLS)
    is_fringe = jnp.any(hits, axis=1)[None, :, None]
    forcing = jnp.where(is_fringe, placed - state_blocks, rhs_blocks)
    forcing = forcing.reshape(width, planes, cells)

    zero_lower = []
    value = jnp.zeros((width, cells), jnp.float32)
    for index in range(planes):
        value = apply_block(
            dinv[:, :, index], forcing[:, index] + apply_block(lower_jac[:, :, index], value)
        )
        zero_lower.append(value)
    value = jnp.zeros((width, cells), jnp.float32)
    for index in range(planes - 1, -1, -1):
        value = zero_lower[index] + apply_block(
            dinv[:, :, index], apply_block(upper_jac[:, :, index], value)
        )
    offsets_here = jnp.stack([zero_lower[planes - 1], value]).reshape((2, width) + tile)
    spread = jnp.broadcast_to(offsets_here[None], (peers,) + offsets_here.shape)
    every = lax.all_to_all(spread, "slab", 0, 0, tiled=True)

    every = every.reshape((peers, 2 * width) + tile)
    index = jnp.reshape(slab_index, (1,)).astype(jnp.int32)
    entries = fold_entries(index, all_maps, every).reshape(2, width, cells)
    low_entry = entries[0]
    up_entry = entries[1]

    lower_planes = []
    value = low_entry
    for index in range(planes):
        value = apply_block(
            dinv[:, :, index], forcing[:, index] + apply_block(lower_jac[:, :, index], value)
        )
        lower_planes.append(value)
    result = [None] * planes
    value = up_entry
    for index in range(planes - 1, -1, -1):
        value = lower_planes[index] + apply_block(
            dinv[:, :, index], apply_block(upper_jac[:, :, index], value)
        )
        result[index] = value
    return jnp.stack(result, axis=1)


def solution(mesh):
    return jax.shard_map(
        sweep_body,
        mesh=mesh,
        in_specs=(
            P(None, "slab", "cross"),
            P(None, "slab", "cross"),
            P(None, None, "slab", "cross"),
            P(None, None, "slab", "cross"),
            P(None, None, "slab", "cross"),
            P(("slab", "cross"), None),
            P(("slab", "cross")),
            P(None, ("slab", "cross")),
            P(None, ("slab", "cross")),
            P(("slab", "cross"), None),
        ),
        out_specs=P(None, "slab", "cross"),
        check_vma=False,
    )
```

```python
import jax
import jax.numpy as jnp
from jax import lax
from jax.experimental import pallas as pl
from jax.experimental.pallas import tpu as pltpu
from jax.sharding import PartitionSpec as P

BLOCK_CELLS = 128


def apply_block(matrix, vector):
    return jnp.sum(matrix * vector[None], axis=1)


def chain_blocks(later, earlier):
    return jnp.sum(later[:, :, None] * earlier[None], axis=1)


def owner_kernel(request_ref, table_ref, out_ref):
    corners = request_ref.shape[0] // 2
    rows = out_ref.shape[0]
    blocks = table_ref.shape[0] // rows
    chunk = 512
    table = table_ref[...]
    lanes = lax.broadcasted_iota(jnp.int32, (BLOCK_CELLS, chunk), 0).astype(jnp.float32)
    for part in range(request_ref.shape[1] // chunk):
        window = pl.ds(part * chunk, chunk)
        wanted = request_ref[0:corners, window]
        wts = request_ref[corners : 2 * corners, window]
        block = jnp.floor(wanted[0:1] * (1.0 / BLOCK_CELLS))
        spread = jnp.where(wanted[0:1] - block * BLOCK_CELLS == lanes, wts[0:1], 0.0)
        for k in range(1, corners):
            offs = wanted[k : k + 1] - block * BLOCK_CELLS
            spread = spread + jnp.where(offs == lanes, wts[k : k + 1], 0.0)
        every = jnp.dot(
            table, spread, precision=lax.Precision.HIGH, preferred_element_type=jnp.float32
        )
        total = jnp.where(block == 0.0, every[0:rows], 0.0)
        for at in range(1, blocks):
            total = total + jnp.where(block == float(at), every[at * rows : (at + 1) * rows], 0.0)
        out_ref[:, window] = total


def interpolate_at_owner(state_flat, request):
    width, resident = state_flat.shape
    blocks = resident // BLOCK_CELLS
    rows = 8
    table = state_flat.reshape(width, blocks, BLOCK_CELLS).transpose(1, 0, 2)
    table = jnp.pad(table, ((0, 0), (0, rows - width), (0, 0))).reshape(blocks * rows, BLOCK_CELLS)
    vmem = pltpu.MemorySpace.VMEM
    out = pl.pallas_call(
        owner_kernel,
        out_shape=jax.ShapeDtypeStruct((rows, request.shape[1]), jnp.float32),
        in_specs=[pl.BlockSpec(memory_space=vmem), pl.BlockSpec(memory_space=vmem)],
        out_specs=pl.BlockSpec(memory_space=vmem),
    )(request, table)
    return out[:width]


def fold_kernel(index_ref, maps_hbm, offsets_ref, out_ref, up_ref, maps_ref, arrived):
    peers = maps_ref.shape[0]
    width = out_ref.shape[1]
    square = width * width
    here = index_ref[0]
    zero = offsets_ref[0, 0] * 0.0

    def copy(at):
        return pltpu.make_async_copy(maps_hbm.at[at], maps_ref.at[at], arrived.at[at])

    for at in range(peers):
        copy(at).start()

    def matvec(at, base, vector):
        rows = []
        for i in range(width):
            total = maps_ref[at, base + i * width] * vector[0]
            for j in range(1, width):
                total = total + maps_ref[at, base + i * width + j] * vector[j]
            rows.append(total)
        return rows

    def lower_step(at, carry):
        copy(at).wait()
        entry, kept = carry
        hit = at == here
        kept = tuple(jnp.where(hit, e, k) for e, k in zip(entry, kept))
        response = matvec(at, 2 * square, entry)
        for i in range(width):
            up_ref[at, i] = offsets_ref[at, width + i] + response[i]
        moved = matvec(at, 0, entry)
        entry = tuple(moved[i] + offsets_ref[at, i] for i in range(width))
        return entry, kept

    start = (tuple([zero] * width), tuple([zero] * width))
    _, low = lax.fori_loop(0, peers, lower_step, start, unroll=True)

    def upper_step(step, carry):
        at = peers - 1 - step
        entry, kept = carry
        hit = at == here
        kept = tuple(jnp.where(hit, e, k) for e, k in zip(entry, kept))
        moved = matvec(at, square, entry)
        entry = tuple(moved[i] + up_ref[at, i] for i in range(width))
        return entry, kept

    _, up = lax.fori_loop(0, peers, upper_step, start, unroll=True)
    for i in range(width):
        out_ref[0, i] = low[i]
        out_ref[1, i] = up[i]


def fold_entries(index, all_maps, every):
    peers, _, sub, lanes = all_maps.shape
    width = every.shape[1] // 2
    vmem = pltpu.MemorySpace.VMEM
    return pl.pallas_call(
        fold_kernel,
        out_shape=jax.ShapeDtypeStruct((2, width, sub, lanes), jnp.float32),
        in_specs=[
            pl.BlockSpec(memory_space=pltpu.MemorySpace.SMEM),
            pl.BlockSpec(memory_space=pl.ANY),
            pl.BlockSpec(memory_space=vmem),
        ],
        out_specs=pl.BlockSpec(memory_space=vmem),
        scratch_shapes=[
            pltpu.VMEM((peers, width, sub, lanes), jnp.float32),
            pltpu.VMEM(all_maps.shape, jnp.float32),
            pltpu.SemaphoreType.DMA((peers,)),
        ],
        compiler_params=pltpu.CompilerParams(vmem_limit_bytes=48 * 1024 * 1024),
    )(index, all_maps, every)


def sweep_body(
    state, rhs, dinv, lower_jac, upper_jac, owner, donor_block, offsets, weights, receptor_perm
):
    width, planes, cells = state.shape
    resident_cells = planes * cells
    state_flat = state.reshape(width, resident_cells)
    devices = lax.axis_size(("slab", "cross"))
    slab_index = lax.axis_index("slab")
    fringe_rows = owner.shape[0]
    capacity = 4 * fringe_rows // devices
    blocks = resident_cells // BLOCK_CELLS
    square = width * width

    tile = (cells // BLOCK_CELLS, BLOCK_CELLS)
    tiled_dinv = dinv.reshape((width, width, planes) + tile)
    tiled_lower = lower_jac.reshape((width, width, planes) + tile)
    tiled_upper = upper_jac.reshape((width, width, planes) + tile)
    partial = []
    transfer = None
    for index in range(planes):
        step = chain_blocks(tiled_dinv[:, :, index], tiled_lower[:, :, index])
        transfer = step if transfer is None else chain_blocks(step, transfer)
        partial.append(transfer)
    low_map = transfer
    up_steps = [
        chain_blocks(tiled_dinv[:, :, index], tiled_upper[:, :, index])
        for index in range(planes)
    ]
    up_map = None
    response = partial[planes - 1]
    for index in range(planes - 1, -1, -1):
        up_map = up_steps[index] if up_map is None else chain_blocks(up_steps[index], up_map)
        if index < planes - 1:
            response = partial[index] + chain_blocks(up_steps[index], response)
    maps = jnp.concatenate(
        [m.reshape((square,) + tile) for m in (low_map, up_map, response)], axis=0
    )
    all_maps = lax.all_gather(maps, "slab")
    peers = all_maps.shape[0]

    target = owner[:, 0]
    onehot = (target[:, None] == jnp.arange(devices, dtype=jnp.int32)[None, :]).astype(jnp.int32)
    slot = jnp.sum(jnp.cumsum(onehot, axis=0) * onehot, axis=1) - 1
    flat_slot = target * capacity + slot
    cells_wanted = donor_block[None, :] * BLOCK_CELLS + offsets
    payload = jnp.concatenate([cells_wanted.astype(jnp.float32), weights], axis=0)
    request = jnp.zeros((payload.shape[0], devices * capacity), jnp.float32)
    request = request.at[:, flat_slot].set(payload).reshape(-1, devices, capacity)
    received = lax.all_to_all(request, ("slab", "cross"), split_axis=1, concat_axis=1, tiled=True)
    answer = interpolate_at_owner(state_flat, received.reshape(received.shape[0], -1))
    answer = answer.reshape(width, devices, capacity)
    arrived = lax.all_to_all(answer, ("slab", "cross"), split_axis=1, concat_axis=1, tiled=True)
    interp = jnp.take(arrived.reshape(width, devices * capacity), flat_slot, axis=1)

    fringe_blocks = fringe_rows // BLOCK_CELLS
    chosen = receptor_perm[0, :fringe_blocks]
    hits = chosen[None, :] == jnp.arange(blocks, dtype=jnp.int32)[:, None]
    interp_blocks = interp.reshape(width, fringe_blocks, BLOCK_CELLS)
    placed = jnp.sum(
        jnp.where(hits[None, :, :, None], interp_blocks[:, None, :, :], 0.0), axis=2
    )
    state_blocks = state_flat.reshape(width, blocks, BLOCK_CELLS)
    rhs_blocks = rhs.reshape(width, blocks, BLOCK_CELLS)
    is_fringe = jnp.any(hits, axis=1)[None, :, None]
    forcing = jnp.where(is_fringe, placed - state_blocks, rhs_blocks)
    forcing = forcing.reshape(width, planes, cells)

    zero_lower = []
    value = jnp.zeros((width, cells), jnp.float32)
    for index in range(planes):
        value = apply_block(
            dinv[:, :, index], forcing[:, index] + apply_block(lower_jac[:, :, index], value)
        )
        zero_lower.append(value)
    value = jnp.zeros((width, cells), jnp.float32)
    for index in range(planes - 1, -1, -1):
        value = zero_lower[index] + apply_block(
            dinv[:, :, index], apply_block(upper_jac[:, :, index], value)
        )
    offsets_here = jnp.stack([zero_lower[planes - 1], value]).reshape((2, width) + tile)
    spread = jnp.broadcast_to(offsets_here[None], (peers,) + offsets_here.shape)
    every = lax.all_to_all(spread, "slab", 0, 0, tiled=True)

    every = every.reshape((peers, 2 * width) + tile)
    index = jnp.reshape(slab_index, (1,)).astype(jnp.int32)
    entries = fold_entries(index, all_maps, every).reshape(2, width, cells)
    low_entry = entries[0]
    up_entry = entries[1]

    lower_planes = []
    value = low_entry
    for index in range(planes):
        value = apply_block(
            dinv[:, :, index], forcing[:, index] + apply_block(lower_jac[:, :, index], value)
        )
        lower_planes.append(value)
    result = [None] * planes
    value = up_entry
    for index in range(planes - 1, -1, -1):
        value = lower_planes[index] + apply_block(
            dinv[:, :, index], apply_block(upper_jac[:, :, index], value)
        )
        result[index] = value
    return jnp.stack(result, axis=1)


def solution(mesh):
    return jax.shard_map(
        sweep_body,
        mesh=mesh,
        in_specs=(
            P(None, "slab", "cross"),
            P(None, "slab", "cross"),
            P(None, None, "slab", "cross"),
            P(None, None, "slab", "cross"),
            P(None, None, "slab", "cross"),
            P(("slab", "cross"), None),
            P(("slab", "cross")),
            P(None, ("slab", "cross")),
            P(None, ("slab", "cross")),
            P(("slab", "cross"), None),
        ),
        out_specs=P(None, "slab", "cross"),
        check_vma=False,
    )
```

```python
import jax
import jax.numpy as jnp
from jax import lax
from jax.experimental import pallas as pl
from jax.experimental.pallas import tpu as pltpu
from jax.sharding import PartitionSpec as P

BLOCK_CELLS = 128


def apply_block(matrix, vector):
    return jnp.sum(matrix * vector[None], axis=1)


def chain_blocks(later, earlier):
    return jnp.sum(later[:, :, None] * earlier[None], axis=1)


def owner_kernel(request_ref, table_ref, out_ref):
    corners = request_ref.shape[0] // 2
    rows = out_ref.shape[0]
    blocks = table_ref.shape[0] // rows
    chunk = 512
    table = table_ref[...]
    lanes = lax.broadcasted_iota(jnp.int32, (BLOCK_CELLS, chunk), 0).astype(jnp.float32)
    for part in range(request_ref.shape[1] // chunk):
        window = pl.ds(part * chunk, chunk)
        wanted = request_ref[0:corners, window]
        wts = request_ref[corners : 2 * corners, window]
        block = jnp.floor(wanted[0:1] * (1.0 / BLOCK_CELLS))
        spread = jnp.where(wanted[0:1] - block * BLOCK_CELLS == lanes, wts[0:1], 0.0)
        for k in range(1, corners):
            offs = wanted[k : k + 1] - block * BLOCK_CELLS
            spread = spread + jnp.where(offs == lanes, wts[k : k + 1], 0.0)
        every = jnp.dot(
            table, spread, precision=lax.Precision.HIGH, preferred_element_type=jnp.float32
        )
        total = jnp.where(block == 0.0, every[0:rows], 0.0)
        for at in range(1, blocks):
            total = total + jnp.where(block == float(at), every[at * rows : (at + 1) * rows], 0.0)
        out_ref[:, window] = total


def interpolate_at_owner(state_flat, request):
    width, resident = state_flat.shape
    blocks = resident // BLOCK_CELLS
    rows = 8
    table = state_flat.reshape(width, blocks, BLOCK_CELLS).transpose(1, 0, 2)
    table = jnp.pad(table, ((0, 0), (0, rows - width), (0, 0))).reshape(blocks * rows, BLOCK_CELLS)
    vmem = pltpu.MemorySpace.VMEM
    out = pl.pallas_call(
        owner_kernel,
        out_shape=jax.ShapeDtypeStruct((rows, request.shape[1]), jnp.float32),
        in_specs=[pl.BlockSpec(memory_space=vmem), pl.BlockSpec(memory_space=vmem)],
        out_specs=pl.BlockSpec(memory_space=vmem),
    )(request, table)
    return out[:width]


def fold_kernel(index_ref, maps_hbm, offsets_ref, out_ref, up_ref, maps_ref, arrived):
    peers = maps_ref.shape[0]
    width = out_ref.shape[1]
    square = width * width
    here = index_ref[0]
    zero = offsets_ref[0, 0] * 0.0

    def copy(at):
        return pltpu.make_async_copy(maps_hbm.at[at], maps_ref.at[at], arrived.at[at])

    for at in range(peers):
        copy(at).start()

    def matvec(at, base, vector):
        rows = []
        for i in range(width):
            terms = [maps_ref[at, base + i * width + j] * vector[j] for j in range(width)]
            while len(terms) > 1:
                paired = [terms[k] + terms[k + 1] for k in range(0, len(terms) - 1, 2)]
                terms = paired + terms[len(paired) * 2 :]
            rows.append(terms[0])
        return rows

    def lower_step(at, carry):
        copy(at).wait()
        entry, kept = carry
        hit = at == here
        kept = tuple(jnp.where(hit, e, k) for e, k in zip(entry, kept))
        response = matvec(at, 2 * square, entry)
        for i in range(width):
            up_ref[at, i] = offsets_ref[at, width + i] + response[i]
        moved = matvec(at, 0, entry)
        entry = tuple(moved[i] + offsets_ref[at, i] for i in range(width))
        return entry, kept

    start = (tuple([zero] * width), tuple([zero] * width))
    _, low = lax.fori_loop(0, peers, lower_step, start, unroll=True)

    def upper_step(step, carry):
        at = peers - 1 - step
        entry, kept = carry
        hit = at == here
        kept = tuple(jnp.where(hit, e, k) for e, k in zip(entry, kept))
        moved = matvec(at, square, entry)
        entry = tuple(moved[i] + up_ref[at, i] for i in range(width))
        return entry, kept

    _, up = lax.fori_loop(0, peers, upper_step, start, unroll=True)
    for i in range(width):
        out_ref[0, i] = low[i]
        out_ref[1, i] = up[i]


def fold_entries(index, all_maps, every):
    peers, _, sub, lanes = all_maps.shape
    width = every.shape[1] // 2
    vmem = pltpu.MemorySpace.VMEM
    return pl.pallas_call(
        fold_kernel,
        out_shape=jax.ShapeDtypeStruct((2, width, sub, lanes), jnp.float32),
        in_specs=[
            pl.BlockSpec(memory_space=pltpu.MemorySpace.SMEM),
            pl.BlockSpec(memory_space=pl.ANY),
            pl.BlockSpec(memory_space=vmem),
        ],
        out_specs=pl.BlockSpec(memory_space=vmem),
        scratch_shapes=[
            pltpu.VMEM((peers, width, sub, lanes), jnp.float32),
            pltpu.VMEM(all_maps.shape, jnp.float32),
            pltpu.SemaphoreType.DMA((peers,)),
        ],
        compiler_params=pltpu.CompilerParams(vmem_limit_bytes=48 * 1024 * 1024),
    )(index, all_maps, every)


def sweep_body(
    state, rhs, dinv, lower_jac, upper_jac, owner, donor_block, offsets, weights, receptor_perm
):
    width, planes, cells = state.shape
    resident_cells = planes * cells
    state_flat = state.reshape(width, resident_cells)
    devices = lax.axis_size(("slab", "cross"))
    slab_index = lax.axis_index("slab")
    fringe_rows = owner.shape[0]
    capacity = 4 * fringe_rows // devices
    blocks = resident_cells // BLOCK_CELLS
    square = width * width

    tile = (cells // BLOCK_CELLS, BLOCK_CELLS)
    tiled_dinv = dinv.reshape((width, width, planes) + tile)
    tiled_lower = lower_jac.reshape((width, width, planes) + tile)
    tiled_upper = upper_jac.reshape((width, width, planes) + tile)
    partial = []
    transfer = None
    for index in range(planes):
        step = chain_blocks(tiled_dinv[:, :, index], tiled_lower[:, :, index])
        transfer = step if transfer is None else chain_blocks(step, transfer)
        partial.append(transfer)
    low_map = transfer
    up_steps = [
        chain_blocks(tiled_dinv[:, :, index], tiled_upper[:, :, index])
        for index in range(planes)
    ]
    up_map = None
    response = partial[planes - 1]
    for index in range(planes - 1, -1, -1):
        up_map = up_steps[index] if up_map is None else chain_blocks(up_steps[index], up_map)
        if index < planes - 1:
            response = partial[index] + chain_blocks(up_steps[index], response)
    maps = jnp.concatenate(
        [m.reshape((square,) + tile) for m in (low_map, up_map, response)], axis=0
    )
    all_maps = lax.all_gather(maps, "slab")
    peers = all_maps.shape[0]

    target = owner[:, 0]
    onehot = (target[:, None] == jnp.arange(devices, dtype=jnp.int32)[None, :]).astype(jnp.int32)
    slot = jnp.sum(jnp.cumsum(onehot, axis=0) * onehot, axis=1) - 1
    flat_slot = target * capacity + slot
    cells_wanted = donor_block[None, :] * BLOCK_CELLS + offsets
    payload = jnp.concatenate([cells_wanted.astype(jnp.float32), weights], axis=0)
    request = jnp.zeros((payload.shape[0], devices * capacity), jnp.float32)
    request = request.at[:, flat_slot].set(
        payload, unique_indices=True, mode="promise_in_bounds"
    )
    request = request.reshape(-1, devices, capacity)
    received = lax.all_to_all(request, ("slab", "cross"), split_axis=1, concat_axis=1, tiled=True)
    answer = interpolate_at_owner(state_flat, received.reshape(received.shape[0], -1))
    answer = answer.reshape(width, devices, capacity)
    arrived = lax.all_to_all(answer, ("slab", "cross"), split_axis=1, concat_axis=1, tiled=True)
    interp = arrived.reshape(width, devices * capacity).at[:, flat_slot].get(
        mode="promise_in_bounds", unique_indices=True
    )

    fringe_blocks = fringe_rows // BLOCK_CELLS
    chosen = receptor_perm[0, :fringe_blocks]
    hits = chosen[None, :] == jnp.arange(blocks, dtype=jnp.int32)[:, None]
    interp_blocks = interp.reshape(width, fringe_blocks, BLOCK_CELLS)
    placed = jnp.sum(
        jnp.where(hits[None, :, :, None], interp_blocks[:, None, :, :], 0.0), axis=2
    )
    state_blocks = state_flat.reshape(width, blocks, BLOCK_CELLS)
    rhs_blocks = rhs.reshape(width, blocks, BLOCK_CELLS)
    is_fringe = jnp.any(hits, axis=1)[None, :, None]
    forcing = jnp.where(is_fringe, placed - state_blocks, rhs_blocks)
    forcing = forcing.reshape(width, planes, cells)

    zero_lower = []
    value = jnp.zeros((width, cells), jnp.float32)
    for index in range(planes):
        value = apply_block(
            dinv[:, :, index], forcing[:, index] + apply_block(lower_jac[:, :, index], value)
        )
        zero_lower.append(value)
    value = jnp.zeros((width, cells), jnp.float32)
    for index in range(planes - 1, -1, -1):
        value = zero_lower[index] + apply_block(
            dinv[:, :, index], apply_block(upper_jac[:, :, index], value)
        )
    offsets_here = jnp.stack([zero_lower[planes - 1], value]).reshape((2, width) + tile)
    spread = jnp.broadcast_to(offsets_here[None], (peers,) + offsets_here.shape)
    every = lax.all_to_all(spread, "slab", 0, 0, tiled=True)

    every = every.reshape((peers, 2 * width) + tile)
    index = jnp.reshape(slab_index, (1,)).astype(jnp.int32)
    entries = fold_entries(index, all_maps, every).reshape(2, width, cells)
    low_entry = entries[0]
    up_entry = entries[1]

    lower_planes = []
    value = low_entry
    for index in range(planes):
        value = apply_block(
            dinv[:, :, index], forcing[:, index] + apply_block(lower_jac[:, :, index], value)
        )
        lower_planes.append(value)
    result = [None] * planes
    value = up_entry
    for index in range(planes - 1, -1, -1):
        value = lower_planes[index] + apply_block(
            dinv[:, :, index], apply_block(upper_jac[:, :, index], value)
        )
        result[index] = value
    return jnp.stack(result, axis=1)


def solution(mesh):
    return jax.shard_map(
        sweep_body,
        mesh=mesh,
        in_specs=(
            P(None, "slab", "cross"),
            P(None, "slab", "cross"),
            P(None, None, "slab", "cross"),
            P(None, None, "slab", "cross"),
            P(None, None, "slab", "cross"),
            P(("slab", "cross"), None),
            P(("slab", "cross")),
            P(None, ("slab", "cross")),
            P(None, ("slab", "cross")),
            P(("slab", "cross"), None),
        ),
        out_specs=P(None, "slab", "cross"),
        check_vma=False,
    )
```

```python
import jax
import jax.numpy as jnp
from jax import lax
from jax.experimental import pallas as pl
from jax.experimental.pallas import tpu as pltpu
from jax.sharding import PartitionSpec as P

BLOCK_CELLS = 128


def apply_block(matrix, vector):
    return jnp.sum(matrix * vector[None], axis=1)


def chain_blocks(later, earlier):
    return jnp.sum(later[:, :, None] * earlier[None], axis=1)


def owner_kernel(request_ref, table_ref, out_ref):
    corners = request_ref.shape[0] // 2
    rows = out_ref.shape[0]
    blocks = table_ref.shape[0] // rows
    chunk = 256
    table = table_ref[...]
    lanes = lax.broadcasted_iota(jnp.int32, (BLOCK_CELLS, chunk), 0).astype(jnp.float32)
    for part in range(request_ref.shape[1] // chunk):
        window = pl.ds(part * chunk, chunk)
        wanted = request_ref[0:corners, window]
        wts = request_ref[corners : 2 * corners, window]
        block = jnp.floor(wanted[0:1] * (1.0 / BLOCK_CELLS))
        spread = jnp.where(wanted[0:1] - block * BLOCK_CELLS == lanes, wts[0:1], 0.0)
        for k in range(1, corners):
            offs = wanted[k : k + 1] - block * BLOCK_CELLS
            spread = spread + jnp.where(offs == lanes, wts[k : k + 1], 0.0)
        every = jnp.dot(
            table, spread, precision=lax.Precision.HIGH, preferred_element_type=jnp.float32
        )
        total = jnp.where(block == 0.0, every[0:rows], 0.0)
        for at in range(1, blocks):
            total = total + jnp.where(block == float(at), every[at * rows : (at + 1) * rows], 0.0)
        out_ref[:, window] = total


def interpolate_at_owner(state_flat, request):
    width, resident = state_flat.shape
    blocks = resident // BLOCK_CELLS
    rows = 8
    table = state_flat.reshape(width, blocks, BLOCK_CELLS).transpose(1, 0, 2)
    table = jnp.pad(table, ((0, 0), (0, rows - width), (0, 0))).reshape(blocks * rows, BLOCK_CELLS)
    vmem = pltpu.MemorySpace.VMEM
    out = pl.pallas_call(
        owner_kernel,
        out_shape=jax.ShapeDtypeStruct((rows, request.shape[1]), jnp.float32),
        in_specs=[pl.BlockSpec(memory_space=vmem), pl.BlockSpec(memory_space=vmem)],
        out_specs=pl.BlockSpec(memory_space=vmem),
    )(request, table)
    return out[:width]


def fold_kernel(index_ref, maps_hbm, offsets_ref, out_ref, up_ref, maps_ref, arrived):
    peers = maps_ref.shape[0]
    width = out_ref.shape[1]
    square = width * width
    here = index_ref[0]
    zero = offsets_ref[0, 0] * 0.0

    def copy(at):
        return pltpu.make_async_copy(maps_hbm.at[at], maps_ref.at[at], arrived.at[at])

    for at in range(peers):
        copy(at).start()

    def matvec(at, base, vector):
        rows = []
        for i in range(width):
            terms = [maps_ref[at, base + i * width + j] * vector[j] for j in range(width)]
            while len(terms) > 1:
                paired = [terms[k] + terms[k + 1] for k in range(0, len(terms) - 1, 2)]
                terms = paired + terms[len(paired) * 2 :]
            rows.append(terms[0])
        return rows

    def lower_step(at, carry):
        copy(at).wait()
        entry, kept = carry
        hit = at == here
        kept = tuple(jnp.where(hit, e, k) for e, k in zip(entry, kept))
        response = matvec(at, 2 * square, entry)
        for i in range(width):
            up_ref[at, i] = offsets_ref[at, width + i] + response[i]
        moved = matvec(at, 0, entry)
        entry = tuple(moved[i] + offsets_ref[at, i] for i in range(width))
        return entry, kept

    start = (tuple([zero] * width), tuple([zero] * width))
    _, low = lax.fori_loop(0, peers, lower_step, start, unroll=True)

    def upper_step(step, carry):
        at = peers - 1 - step
        entry, kept = carry
        hit = at == here
        kept = tuple(jnp.where(hit, e, k) for e, k in zip(entry, kept))
        moved = matvec(at, square, entry)
        entry = tuple(moved[i] + up_ref[at, i] for i in range(width))
        return entry, kept

    _, up = lax.fori_loop(0, peers, upper_step, start, unroll=True)
    for i in range(width):
        out_ref[0, i] = low[i]
        out_ref[1, i] = up[i]


def fold_entries(index, all_maps, every):
    peers, _, sub, lanes = all_maps.shape
    width = every.shape[1] // 2
    vmem = pltpu.MemorySpace.VMEM
    return pl.pallas_call(
        fold_kernel,
        out_shape=jax.ShapeDtypeStruct((2, width, sub, lanes), jnp.float32),
        in_specs=[
            pl.BlockSpec(memory_space=pltpu.MemorySpace.SMEM),
            pl.BlockSpec(memory_space=pl.ANY),
            pl.BlockSpec(memory_space=vmem),
        ],
        out_specs=pl.BlockSpec(memory_space=vmem),
        scratch_shapes=[
            pltpu.VMEM((peers, width, sub, lanes), jnp.float32),
            pltpu.VMEM(all_maps.shape, jnp.float32),
            pltpu.SemaphoreType.DMA((peers,)),
        ],
        compiler_params=pltpu.CompilerParams(vmem_limit_bytes=48 * 1024 * 1024),
    )(index, all_maps, every)


def sweep_body(
    state, rhs, dinv, lower_jac, upper_jac, owner, donor_block, offsets, weights, receptor_perm
):
    width, planes, cells = state.shape
    resident_cells = planes * cells
    state_flat = state.reshape(width, resident_cells)
    devices = lax.axis_size(("slab", "cross"))
    slab_index = lax.axis_index("slab")
    fringe_rows = owner.shape[0]
    capacity = 4 * fringe_rows // devices
    blocks = resident_cells // BLOCK_CELLS
    square = width * width

    tile = (cells // BLOCK_CELLS, BLOCK_CELLS)
    tiled_dinv = dinv.reshape((width, width, planes) + tile)
    tiled_lower = lower_jac.reshape((width, width, planes) + tile)
    tiled_upper = upper_jac.reshape((width, width, planes) + tile)
    partial = []
    transfer = None
    for index in range(planes):
        step = chain_blocks(tiled_dinv[:, :, index], tiled_lower[:, :, index])
        transfer = step if transfer is None else chain_blocks(step, transfer)
        partial.append(transfer)
    low_map = transfer
    up_steps = [
        chain_blocks(tiled_dinv[:, :, index], tiled_upper[:, :, index])
        for index in range(planes)
    ]
    up_map = None
    response = partial[planes - 1]
    for index in range(planes - 1, -1, -1):
        up_map = up_steps[index] if up_map is None else chain_blocks(up_steps[index], up_map)
        if index < planes - 1:
            response = partial[index] + chain_blocks(up_steps[index], response)
    maps = jnp.concatenate(
        [m.reshape((square,) + tile) for m in (low_map, up_map, response)], axis=0
    )
    all_maps = lax.all_gather(maps, "slab")
    peers = all_maps.shape[0]

    target = owner[:, 0]
    onehot = (target[:, None] == jnp.arange(devices, dtype=jnp.int32)[None, :]).astype(jnp.int32)
    slot = jnp.sum(jnp.cumsum(onehot, axis=0) * onehot, axis=1) - 1
    flat_slot = target * capacity + slot
    cells_wanted = donor_block[None, :] * BLOCK_CELLS + offsets
    payload = jnp.concatenate([cells_wanted.astype(jnp.float32), weights], axis=0)
    request = jnp.zeros((payload.shape[0], devices * capacity), jnp.float32)
    request = request.at[:, flat_slot].set(payload).reshape(-1, devices, capacity)
    received = lax.all_to_all(request, ("slab", "cross"), split_axis=1, concat_axis=1, tiled=True)
    answer = interpolate_at_owner(state_flat, received.reshape(received.shape[0], -1))
    answer = answer.reshape(width, devices, capacity)
    arrived = lax.all_to_all(answer, ("slab", "cross"), split_axis=1, concat_axis=1, tiled=True)
    interp = jnp.take(arrived.reshape(width, devices * capacity), flat_slot, axis=1)

    fringe_blocks = fringe_rows // BLOCK_CELLS
    chosen = receptor_perm[0, :fringe_blocks]
    hits = chosen[None, :] == jnp.arange(blocks, dtype=jnp.int32)[:, None]
    interp_blocks = interp.reshape(width, fringe_blocks, BLOCK_CELLS)
    placed = jnp.sum(
        jnp.where(hits[None, :, :, None], interp_blocks[:, None, :, :], 0.0), axis=2
    )
    state_blocks = state_flat.reshape(width, blocks, BLOCK_CELLS)
    rhs_blocks = rhs.reshape(width, blocks, BLOCK_CELLS)
    is_fringe = jnp.any(hits, axis=1)[None, :, None]
    forcing = jnp.where(is_fringe, placed - state_blocks, rhs_blocks)
    forcing = forcing.reshape(width, planes, cells)

    zero_lower = []
    value = jnp.zeros((width, cells), jnp.float32)
    for index in range(planes):
        value = apply_block(
            dinv[:, :, index], forcing[:, index] + apply_block(lower_jac[:, :, index], value)
        )
        zero_lower.append(value)
    value = jnp.zeros((width, cells), jnp.float32)
    for index in range(planes - 1, -1, -1):
        value = zero_lower[index] + apply_block(
            dinv[:, :, index], apply_block(upper_jac[:, :, index], value)
        )
    offsets_here = jnp.stack([zero_lower[planes - 1], value]).reshape((2, width) + tile)
    spread = jnp.broadcast_to(offsets_here[None], (peers,) + offsets_here.shape)
    every = lax.all_to_all(spread, "slab", 0, 0, tiled=True)

    every = every.reshape((peers, 2 * width) + tile)
    index = jnp.reshape(slab_index, (1,)).astype(jnp.int32)
    entries = fold_entries(index, all_maps, every).reshape(2, width, cells)
    low_entry = entries[0]
    up_entry = entries[1]

    lower_planes = []
    value = low_entry
    for index in range(planes):
        value = apply_block(
            dinv[:, :, index], forcing[:, index] + apply_block(lower_jac[:, :, index], value)
        )
        lower_planes.append(value)
    result = [None] * planes
    value = up_entry
    for index in range(planes - 1, -1, -1):
        value = lower_planes[index] + apply_block(
            dinv[:, :, index], apply_block(upper_jac[:, :, index], value)
        )
        result[index] = value
    return jnp.stack(result, axis=1)


def solution(mesh):
    return jax.shard_map(
        sweep_body,
        mesh=mesh,
        in_specs=(
            P(None, "slab", "cross"),
            P(None, "slab", "cross"),
            P(None, None, "slab", "cross"),
            P(None, None, "slab", "cross"),
            P(None, None, "slab", "cross"),
            P(("slab", "cross"), None),
            P(("slab", "cross")),
            P(None, ("slab", "cross")),
            P(None, ("slab", "cross")),
            P(("slab", "cross"), None),
        ),
        out_specs=P(None, "slab", "cross"),
        check_vma=False,
    )
```
